32 devices in a mesh: grp: 2 (over x), row: 4 (over y, core), col: 4 (over z).
Axes of the slice: x: 2, y: 2, z: 4, core: 2. Of those that a mesh axis runs over, the one named last changes fastest.
Arguments:
- patches: bfloat16 [64, 64, 1024], P(('grp', 'row'), 'col'), parts along dimension 0, may hold values from -620 to 620
- upstream: bfloat16 [64, 64, 1024], P(('grp', 'row'), 'col'), parts along dimension 0, may hold values from -0.59765625 to 0.59765625
- qkv_weight: bfloat16 [1024, 3072], P('row'), may hold values from -0.1875 to 0.1875
- out_weight: bfloat16 [1024, 1024], P('row'), may hold values from -0.1875 to 0.1875
- layer_norm_gain: float32 [1024], replicated, may hold values from 0.5 to 1.5
- pos_bias: float32 [16, 49], replicated, may hold values from -3 to 300
- valid_mask: int32 [64, 64], P(('grp', 'row'), 'col'), parts along dimension 0, may hold values 0 or 1
Outputs:
- patch_gradient: float32 [64, 64, 1024], P(('grp', 'row'), 'col'), parts along dimension 0
- qkv_grad: float32 [2048, 3072], P(('grp', 'row')), parts along dimension 0
- out_grad: float32 [2048, 1024], P(('grp', 'row')), parts along dimension 0
- gain_gradient: float32 [2048], P(('grp', 'row')), parts along dimension 0
- bias_grad: float32 [32, 49], P(('grp', 'row')), parts along dimension 0
The draws below stay inside these ranges and needn't reach their ends.
There are 2 independent parts, one for each index of `grp`. The reference program is written for one: setup_inputs(seed, part) draws one part's arguments, and reference() takes and returns one part's arrays. A program takes and returns all parts, laid end to end along the dimension named above; an argument that names none is the same for every part. Nothing has to cross between parts.
All inputs are finite; a program needn't handle non-finite values. No bound on the sum of `valid_mask` on one device may be relied on, other than what follows from the above.
Results may differ from the reference program's by a relative error of at most 0.012.
Values may be sent and summed in bfloat16 or wider, within the bound.
No kernel may reach another device: no remote copies, remote signals or barrier semaphores. Data moves between devices by JAX's collectives and lax.ppermute only.
A program may use at most 192 MiB of HBM per device.

```python
import math
import jax
import jax.numpy as jnp
from jax import lax

D = 1024
HEADS = 16
RAD = 3
HDIM = 64
WIN = 7
H_IMG = 32
W_IMG = 64


def draw_patches(key, part):
    first, second, third = jax.random.split(jax.random.fold_in(key, 11), 3)
    row_scale = jnp.exp(jax.random.uniform(first, (H_IMG, W_IMG, 1), jnp.float32) * math.log(10.0))
    col_scale = jnp.exp(jax.random.uniform(second, (1, 1, D), jnp.float32) * math.log(10.0))
    base = jnp.clip(jax.random.normal(third, (H_IMG, W_IMG, D), jnp.float32), -4.0, 4.0)
    return (base * row_scale * col_scale).astype(jnp.bfloat16)


def draw_pos_bias(key, part):
    first = jax.random.fold_in(jax.random.fold_in(key, 23), 0)
    base = jnp.clip(jax.random.normal(first, (HEADS, WIN * WIN), jnp.float32), -3.0, 3.0)
    return base


def set_ends(drawn, key, least, high):
    extent = drawn.shape
    place = [jax.random.randint(jax.random.fold_in(key, axis), (), 0, extent[axis]) for axis in range(len(extent))]
    drawn = drawn.at[tuple(place)].set(least)
    longest = extent.index(max(extent))
    place[longest] = (place[longest] + 1) % extent[longest]
    return drawn.at[tuple(place)].set(high)


def block_scale(stream_key, extent, cuts, least, top_value):
    loudness, own = 1.0, jax.random.fold_in(stream_key, 6)
    for axis_at, blocks in cuts:
        heights = jnp.exp(jax.random.uniform(jax.random.fold_in(own, axis_at), (blocks,), jnp.float32, least / len(cuts), top_value / len(cuts)))
        loudness = loudness * jnp.repeat(heights, extent[axis_at] // blocks).reshape([-1 if axis == axis_at else 1 for axis in range(len(extent))])
    return loudness


def normal_values(stream_key, dims, deviation, reach, pieces=(), dtype=jnp.bfloat16):
    factor_of = block_scale(stream_key, dims, pieces, -0.22, 0.18) if pieces else 1.0
    array = jax.random.normal(stream_key, dims, jnp.float32) * deviation * factor_of
    return jnp.minimum(jnp.maximum(array, -reach), reach).astype(dtype)


def setup_inputs(seed: int = 0, part: int = 0) -> dict:
    arg_keys = jax.random.split(jax.random.key(seed), 8)
    part_splits = jax.random.split(jax.random.fold_in(arg_keys[7], part), 8)
    patches = draw_patches(jax.random.fold_in(jax.random.fold_in(arg_keys[7], part), 71), part)
    upstream = normal_values(part_splits[1], (H_IMG, W_IMG, D), 0.1, 0.59765625, ((0, 4), (1, 4)))
    qkv_weight = normal_values(arg_keys[2], (D, 3 * D), D ** -0.5, 0.1875, ((0, 4),))
    out_weight = normal_values(arg_keys[3], (D, D), D ** -0.5, 0.1875, ((0, 4),))
    layer_norm_gain = jnp.clip(1.0 + 0.1 * jax.random.normal(arg_keys[4], (D,), jnp.float32), 0.5, 1.5)
    pos_bias = draw_pos_bias(jax.random.fold_in(arg_keys[7], 71), part)
    valid_mask = set_ends((jax.random.randint(part_splits[6], (H_IMG, W_IMG), 0, 8) < 7).astype(jnp.int32), jax.random.fold_in(part_splits[6], 1), 0, 1)
    return dict(patches=patches, upstream=upstream, qkv_weight=qkv_weight, out_weight=out_weight, layer_norm_gain=layer_norm_gain, pos_bias=pos_bias, valid_mask=valid_mask)


def apply_layer_norm(values, norm_gain_value):
    floats = values.astype(jnp.float32)
    feature_mean = lax.optimization_barrier(jnp.mean(floats, axis=-1, keepdims=True))
    mean_removed = floats - feature_mean
    variance = lax.optimization_barrier(jnp.mean(mean_removed * mean_removed, axis=-1, keepdims=True))
    inverse_deviation = lax.rsqrt(variance + 1e-05)
    standardized_input = mean_removed * inverse_deviation
    return ((standardized_input * norm_gain_value).astype(jnp.bfloat16), standardized_input, inverse_deviation)

def head_dot(left, right, heads):
    product = left.astype(jnp.float32) * right.astype(jnp.float32)
    shaped = product.reshape(product.shape[:-1] + (heads, product.shape[-1] // heads))
    return lax.optimization_barrier(jnp.sum(shaped, axis=-1))

def spread(weights, values):
    heads = weights.shape[-1]
    floats = values.astype(jnp.float32)
    shaped = floats.reshape(floats.shape[:-1] + (heads, floats.shape[-1] // heads))
    return (weights[..., None] * shaped).reshape(floats.shape)

def reference(patches, upstream, qkv_weight, out_weight, layer_norm_gain, pos_bias, valid_mask):
    rows, cols, width = patches.shape
    normed_features, standardized_input, inverse_deviation = apply_layer_norm(patches, layer_norm_gain)
    flat = normed_features.reshape(-1, width)
    joined = jnp.dot(flat, qkv_weight, preferred_element_type=jnp.float32).astype(jnp.bfloat16)
    joined = joined.reshape(rows, cols, 3 * width)
    query = joined[..., :width]
    keys = joined[..., width:2 * width]
    values = joined[..., 2 * width:]
    margin = ((RAD, RAD), (RAD, RAD), (0, 0))
    key_pad = jnp.pad(keys, margin)
    value_pad = jnp.pad(values, margin)
    mask_pad = jnp.pad(valid_mask, RAD)
    scale = float(HDIM) ** (-0.5)
    offsets = [(a, b) for a in range(-RAD, RAD + 1) for b in range(-RAD, RAD + 1)]
    centre = RAD * WIN + RAD
    score_list = []
    for index, (a, b) in enumerate(offsets):
        key_slice = key_pad[RAD + a:RAD + a + rows, RAD + b:RAD + b + cols]
        allowed = (mask_pad[RAD + a:RAD + a + rows, RAD + b:RAD + b + cols] == 1) | (index == centre)
        raw = head_dot(query, key_slice, HEADS) * scale + pos_bias[:, index]
        score_list.append(jnp.where(allowed[..., None], raw, -jnp.inf))
    scores = jnp.stack(score_list)
    top = lax.optimization_barrier(jnp.max(scores, axis=0))
    expo = jnp.exp(scores - top)
    probs = expo / lax.optimization_barrier(jnp.sum(expo, axis=0))
    total = jnp.zeros((rows, cols, width), jnp.float32)
    for index, (a, b) in enumerate(offsets):
        total = total + spread(probs[index], value_pad[RAD + a:RAD + a + rows, RAD + b:RAD + b + cols])
    attended = total.astype(jnp.bfloat16)
    grad_flat = upstream.reshape(-1, width)
    out_grad = jnp.dot(attended.reshape(-1, width).T, grad_flat, preferred_element_type=jnp.float32)
    attended_grad = jnp.dot(grad_flat, out_weight.T, preferred_element_type=jnp.float32).astype(jnp.bfloat16)
    attended_grad = attended_grad.reshape(rows, cols, width)
    delta = head_dot(attended_grad, attended, HEADS)
    query_grad = jnp.zeros((rows, cols, width), jnp.float32)
    key_grad_pad = jnp.zeros((rows + 2 * RAD, cols + 2 * RAD, width), jnp.float32)
    value_grad_pad = jnp.zeros((rows + 2 * RAD, cols + 2 * RAD, width), jnp.float32)
    bias_cols = []
    for index, (a, b) in enumerate(offsets):
        key_slice = key_pad[RAD + a:RAD + a + rows, RAD + b:RAD + b + cols]
        value_slice = value_pad[RAD + a:RAD + a + rows, RAD + b:RAD + b + cols]
        score_grad = probs[index] * (head_dot(attended_grad, value_slice, HEADS) - delta)
        bias_cols.append(lax.optimization_barrier(jnp.sum(score_grad, axis=(0, 1))))
        query_grad = query_grad + spread(score_grad, key_slice) * scale
        key_grad_pad = key_grad_pad.at[RAD + a:RAD + a + rows, RAD + b:RAD + b + cols].add(spread(score_grad, query) * scale)
        value_grad_pad = value_grad_pad.at[RAD + a:RAD + a + rows, RAD + b:RAD + b + cols].add(spread(probs[index], attended_grad))
    key_grad = key_grad_pad[RAD:RAD + rows, RAD:RAD + cols]
    value_grad = value_grad_pad[RAD:RAD + rows, RAD:RAD + cols]
    joined_grad = jnp.concatenate([query_grad, key_grad, value_grad], axis=-1).astype(jnp.bfloat16)
    joined_grad = joined_grad.reshape(-1, 3 * width)
    normed_gradient = jnp.dot(joined_grad, qkv_weight.T, preferred_element_type=jnp.float32).reshape(rows, cols, width)
    qkv_grad = jnp.dot(flat.T, joined_grad, preferred_element_type=jnp.float32)
    gain_gradient = lax.optimization_barrier(jnp.sum(normed_gradient * standardized_input, axis=(0, 1)))
    scaled_features = normed_gradient * layer_norm_gain
    patch_gradient = upstream.astype(jnp.float32) + inverse_deviation * (scaled_features - lax.optimization_barrier(jnp.mean(scaled_features, axis=-1, keepdims=True)) - standardized_input * lax.optimization_barrier(jnp.mean(scaled_features * standardized_input, axis=-1, keepdims=True)))
    bias_grad = jnp.stack(bias_cols, axis=1)
    return (patch_gradient, qkv_grad, out_grad, gain_gradient, bias_grad)
```

```python
import jax
import jax.numpy as jnp
from jax import lax
from jax.sharding import PartitionSpec as P

RAD = 3
HIGHEST = lax.Precision.HIGHEST


def extended_2(shard, sides, width):
    for axis, dim in sides:
        devices, length = (lax.axis_size(axis), shard.shape[dim])
        up = [(i, i + 1) for i in range(devices - 1)]
        down = [(j, i) for i, j in up]
        last = lax.slice_in_dim(shard, length - width, length, axis=dim)
        first = lax.slice_in_dim(shard, 0, width, axis=dim)
        before = lax.ppermute(last, axis, up)
        after = lax.ppermute(first, axis, down)
        shard = jnp.concatenate([before, shard, after], axis=dim)
    return shard


def passed_along(value, axis, steps):
    count = lax.axis_size(axis)
    first, last = (max(0, -steps), min(count, count - steps))
    return lax.ppermute(value, axis, [(source, source + steps) for source in range(first, last)])


def apply_layer_norm(values, norm_gain_value):
    floats = values.astype(jnp.float32)
    feature_mean = jnp.mean(floats, axis=-1, keepdims=True)
    mean_removed = floats - feature_mean
    variance = jnp.mean(mean_removed * mean_removed, axis=-1, keepdims=True)
    inverse_deviation = lax.rsqrt(variance + 1e-05)
    standardized_input = mean_removed * inverse_deviation
    return (
        (standardized_input * norm_gain_value).astype(jnp.bfloat16),
        standardized_input,
        inverse_deviation,
    )


def window_tables(rows, cols, reach):
    side = 2 * reach + 1
    shape = (rows, cols, rows + 2 * reach, cols + 2 * reach)
    row_gap = lax.broadcasted_iota(jnp.int32, shape, 2) - lax.broadcasted_iota(jnp.int32, shape, 0)
    col_gap = lax.broadcasted_iota(jnp.int32, shape, 3) - lax.broadcasted_iota(jnp.int32, shape, 1)
    inside = (row_gap >= 0) & (row_gap < side) & (col_gap >= 0) & (col_gap < side)
    offset_id = jnp.where(inside, row_gap * side + col_gap, -1)
    centre = (row_gap == reach) & (col_gap == reach)
    nq = rows * cols
    nk = (rows + 2 * reach) * (cols + 2 * reach)
    offset_id = offset_id.reshape(nq * nk)
    one_hot = (
        offset_id[None, :] == lax.broadcasted_iota(jnp.int32, (side * side, nq * nk), 0)
    ).astype(jnp.float32)
    return inside.reshape(nq, nk), centre.reshape(nq, nk), one_hot


def body(patches, upstream, qkv_weight, out_weight, layer_norm_gain, pos_bias, valid_mask):
    rows, cols, width = patches.shape
    heads = pos_bias.shape[0]
    hdim = width // heads
    reach = RAD
    ext_rows, ext_cols = rows + 2 * reach, cols + 2 * reach
    nq, nk = rows * cols, ext_rows * ext_cols
    scale = float(hdim) ** (-0.5)
    full_qkv, full_out = (
        lax.all_gather(qkv_weight, "row", axis=0, tiled=True),
        lax.all_gather(out_weight, "row", axis=0, tiled=True),
    )
    normed_features, standardized_input, inverse_deviation = apply_layer_norm(
        patches, layer_norm_gain
    )
    flat = normed_features.reshape(-1, width)
    joined = jnp.dot(flat, full_qkv, preferred_element_type=jnp.float32).astype(jnp.bfloat16)
    query = joined[:, :width]
    kv = joined[:, width:].reshape(rows, cols, 2 * width)
    kv_ext = extended_2(kv, (("row", 0), ("col", 1)), reach).reshape(nk, 2 * width)
    mask_ext = extended_2(valid_mask, (("row", 0), ("col", 1)), reach).reshape(nk)
    q3 = query.reshape(nq, heads, hdim)
    k3 = kv_ext[:, :width].reshape(nk, heads, hdim)
    v3 = kv_ext[:, width:].reshape(nk, heads, hdim)

    inside, centre, one_hot = window_tables(rows, cols, reach)
    allowed = inside & ((mask_ext[None, :] == 1) | centre)
    bias_full = jnp.dot(pos_bias, one_hot, precision=HIGHEST).reshape(heads, nq, nk)
    raw = jnp.einsum("phd,khd->hpk", q3, k3, preferred_element_type=jnp.float32)
    scores = jnp.where(allowed[None], raw * scale + bias_full, -jnp.inf)
    top = jnp.max(scores, axis=-1, keepdims=True)
    expo = jnp.exp(scores - top)
    denom = jnp.sum(expo, axis=-1, keepdims=True)
    probs = expo / denom
    attended3 = jnp.einsum(
        "hpk,khd->phd", probs, v3.astype(jnp.float32), precision=HIGHEST,
        preferred_element_type=jnp.float32,
    )
    attended = attended3.astype(jnp.bfloat16).reshape(nq, width)

    grad_flat = upstream.reshape(-1, width)
    out_grad = jnp.dot(attended.T, grad_flat, preferred_element_type=jnp.float32)
    out_sum = lax.psum(
        lax.psum_scatter(out_grad.astype(jnp.bfloat16), "row", scatter_dimension=0, tiled=True), "col"
    ).astype(jnp.float32)
    attended_grad = jnp.dot(grad_flat, full_out.T, preferred_element_type=jnp.float32).astype(
        jnp.bfloat16
    )
    ag3 = attended_grad.reshape(nq, heads, hdim)
    delta = jnp.sum(
        ag3.astype(jnp.float32) * attended.reshape(nq, heads, hdim).astype(jnp.float32), axis=-1
    )
    prob_grad = jnp.einsum("phd,khd->hpk", ag3, v3, preferred_element_type=jnp.float32)
    score_grad = probs * (prob_grad - delta.T[:, :, None])
    bias_term = jnp.dot(
        score_grad.reshape(heads, nq * nk), one_hot.T, precision=HIGHEST,
        preferred_element_type=jnp.float32,
    )
    query_grad = jnp.einsum(
        "hpk,khd->phd", score_grad, k3.astype(jnp.float32), precision=HIGHEST,
        preferred_element_type=jnp.float32,
    ) * scale
    key_ext_grad = jnp.einsum(
        "hpk,phd->khd", score_grad, q3.astype(jnp.float32), precision=HIGHEST,
        preferred_element_type=jnp.float32,
    ) * scale
    value_ext_grad = jnp.einsum(
        "hpk,phd->khd", probs, ag3.astype(jnp.float32), precision=HIGHEST,
        preferred_element_type=jnp.float32,
    )
    buffer = jnp.concatenate(
        [key_ext_grad.reshape(ext_rows, ext_cols, width), value_ext_grad.reshape(ext_rows, ext_cols, width)],
        axis=-1,
    )
    from_below = passed_along(buffer[:reach], "row", -1)
    from_above = passed_along(buffer[reach + rows :], "row", 1)
    middle = buffer[reach : reach + rows]
    middle = middle.at[:reach].add(from_above)
    middle = middle.at[rows - reach :].add(from_below)
    from_right = passed_along(middle[:, :reach].astype(jnp.bfloat16), "col", -1).astype(jnp.float32)
    from_left = passed_along(middle[:, reach + cols :].astype(jnp.bfloat16), "col", 1).astype(
        jnp.float32
    )
    inner = middle[:, reach : reach + cols]
    inner = inner.at[:, :reach].add(from_left)
    inner = inner.at[:, cols - reach :].add(from_right)
    joined_grad = jnp.concatenate(
        [query_grad.reshape(rows, cols, width), inner], axis=-1
    ).astype(jnp.bfloat16)
    joined_grad = joined_grad.reshape(-1, 3 * width)
    normed_gradient = jnp.dot(joined_grad, full_qkv.T, preferred_element_type=jnp.float32).reshape(
        rows, cols, width
    )
    qkv_term = jnp.dot(flat.T, joined_grad, preferred_element_type=jnp.float32)
    gain_product = jnp.sum(normed_gradient * standardized_input, axis=(0, 1))
    scaled_features = normed_gradient * layer_norm_gain
    patch_gradient = upstream.astype(jnp.float32) + inverse_deviation * (
        scaled_features
        - jnp.mean(scaled_features, axis=-1, keepdims=True)
        - standardized_input
        * jnp.mean(scaled_features * standardized_input, axis=-1, keepdims=True)
    )
    row_count = lax.axis_size("row")
    heads_per, rows_per = heads // row_count, width // row_count
    bias_rows = jnp.pad(
        bias_term.reshape(row_count, heads_per, -1), ((0, 0), (0, rows_per - heads_per), (0, 0))
    ).reshape(width, -1)
    offsets = bias_term.shape[1]
    spare = 128 - 1 - offsets
    big = jnp.concatenate(
        [qkv_term, gain_product[:, None], bias_rows, jnp.zeros((width, spare), jnp.float32)], axis=1
    ).astype(jnp.bfloat16)
    big_sum = lax.psum(lax.psum_scatter(big, "row", scatter_dimension=0, tiled=True), "col")
    big_sum = big_sum.astype(jnp.float32)
    qkv_sum = big_sum[:, : 3 * width]
    gain_sum = big_sum[:, 3 * width]
    bias_sum = big_sum[:heads_per, 3 * width + 1 : 3 * width + 1 + offsets]
    return (patch_gradient, qkv_sum, out_sum, gain_sum, bias_sum)


def solution(mesh):
    in_specs = (
        P(("grp", "row"), "col", None),
        P(("grp", "row"), "col", None),
        P("row", None),
        P("row", None),
        P(),
        P(),
        P(("grp", "row"), "col"),
    )
    out_specs = (
        P(("grp", "row"), "col", None),
        P(("grp", "row"), None),
        P(("grp", "row"), None),
        P(("grp", "row")),
        P(("grp", "row"), None),
    )
    return jax.shard_map(body, mesh=mesh, in_specs=in_specs, out_specs=out_specs, check_vma=False)
```

```python
import jax
import jax.numpy as jnp
from jax import lax
from jax.sharding import PartitionSpec as P

RAD = 3
HIGHEST = lax.Precision.HIGHEST


def extended_2(shard, sides, width):
    for axis, dim in sides:
        devices, length = (lax.axis_size(axis), shard.shape[dim])
        up = [(i, i + 1) for i in range(devices - 1)]
        down = [(j, i) for i, j in up]
        last = lax.slice_in_dim(shard, length - width, length, axis=dim)
        first = lax.slice_in_dim(shard, 0, width, axis=dim)
        before = lax.ppermute(last, axis, up)
        after = lax.ppermute(first, axis, down)
        shard = jnp.concatenate([before, shard, after], axis=dim)
    return shard


def passed_along(value, axis, steps):
    count = lax.axis_size(axis)
    first, last = (max(0, -steps), min(count, count - steps))
    return lax.ppermute(value, axis, [(source, source + steps) for source in range(first, last)])


def apply_layer_norm(values, norm_gain_value):
    floats = values.astype(jnp.float32)
    feature_mean = jnp.mean(floats, axis=-1, keepdims=True)
    mean_removed = floats - feature_mean
    variance = jnp.mean(mean_removed * mean_removed, axis=-1, keepdims=True)
    inverse_deviation = lax.rsqrt(variance + 1e-05)
    standardized_input = mean_removed * inverse_deviation
    return (
        (standardized_input * norm_gain_value).astype(jnp.bfloat16),
        standardized_input,
        inverse_deviation,
    )


def window_tables(rows, cols, reach):
    side = 2 * reach + 1
    shape = (rows, cols, rows + 2 * reach, cols + 2 * reach)
    row_gap = lax.broadcasted_iota(jnp.int32, shape, 2) - lax.broadcasted_iota(jnp.int32, shape, 0)
    col_gap = lax.broadcasted_iota(jnp.int32, shape, 3) - lax.broadcasted_iota(jnp.int32, shape, 1)
    inside = (row_gap >= 0) & (row_gap < side) & (col_gap >= 0) & (col_gap < side)
    offset_id = jnp.where(inside, row_gap * side + col_gap, -1)
    centre = (row_gap == reach) & (col_gap == reach)
    nq = rows * cols
    nk = (rows + 2 * reach) * (cols + 2 * reach)
    offset_id = offset_id.reshape(nq * nk)
    one_hot = (
        offset_id[None, :] == lax.broadcasted_iota(jnp.int32, (side * side, nq * nk), 0)
    ).astype(jnp.float32)
    return inside.reshape(nq, nk), centre.reshape(nq, nk), one_hot


def body(patches, upstream, qkv_weight, out_weight, layer_norm_gain, pos_bias, valid_mask):
    rows, cols, width = patches.shape
    heads = pos_bias.shape[0]
    hdim = width // heads
    reach = RAD
    ext_rows, ext_cols = rows + 2 * reach, cols + 2 * reach
    nq, nk = rows * cols, ext_rows * ext_cols
    scale = float(hdim) ** (-0.5)
    full_qkv, full_out = (
        lax.all_gather(qkv_weight, "row", axis=0, tiled=True),
        lax.all_gather(out_weight, "row", axis=0, tiled=True),
    )
    normed_features, standardized_input, inverse_deviation = apply_layer_norm(
        patches, layer_norm_gain
    )
    flat = normed_features.reshape(-1, width)
    joined = jnp.dot(flat, full_qkv, preferred_element_type=jnp.float32).astype(jnp.bfloat16)
    query = joined[:, :width]
    kv = joined[:, width:].reshape(rows, cols, 2 * width)
    kv_ext = extended_2(kv, (("row", 0), ("col", 1)), reach).reshape(nk, 2 * width)
    mask_ext = extended_2(valid_mask, (("row", 0), ("col", 1)), reach).reshape(nk)
    q3 = query.reshape(nq, heads, hdim)
    k3 = kv_ext[:, :width].reshape(nk, heads, hdim)
    v3 = kv_ext[:, width:].reshape(nk, heads, hdim)

    inside, centre, one_hot = window_tables(rows, cols, reach)
    allowed = inside & ((mask_ext[None, :] == 1) | centre)
    bias_full = jnp.dot(pos_bias, one_hot, precision=HIGHEST).reshape(heads, nq, nk)
    raw = jnp.einsum("phd,khd->hpk", q3, k3, preferred_element_type=jnp.float32)
    scores = jnp.where(allowed[None], raw * scale + bias_full, -jnp.inf)
    top = jnp.max(scores, axis=-1, keepdims=True)
    expo = jnp.exp(scores - top)
    denom = jnp.sum(expo, axis=-1, keepdims=True)
    probs = expo / denom
    attended3 = jnp.einsum(
        "hpk,khd->phd", probs, v3.astype(jnp.float32), precision=HIGHEST,
        preferred_element_type=jnp.float32,
    )
    attended = attended3.astype(jnp.bfloat16).reshape(nq, width)

    grad_flat = upstream.reshape(-1, width)
    out_grad = jnp.dot(attended.T, grad_flat, preferred_element_type=jnp.float32)
    out_sum = lax.psum(
        lax.psum_scatter(out_grad.astype(jnp.bfloat16), "row", scatter_dimension=0, tiled=True), "col"
    ).astype(jnp.float32)
    out_sum, flat = lax.optimization_barrier((out_sum, flat))
    attended_grad = jnp.dot(grad_flat, full_out.T, preferred_element_type=jnp.float32).astype(
        jnp.bfloat16
    )
    ag3 = attended_grad.reshape(nq, heads, hdim)
    delta = jnp.sum(
        ag3.astype(jnp.float32) * attended.reshape(nq, heads, hdim).astype(jnp.float32), axis=-1
    )
    prob_grad = jnp.einsum("phd,khd->hpk", ag3, v3, preferred_element_type=jnp.float32)
    score_grad = probs * (prob_grad - delta.T[:, :, None])
    bias_term = jnp.dot(
        score_grad.reshape(heads, nq * nk), one_hot.T, precision=HIGHEST,
        preferred_element_type=jnp.float32,
    )
    query_grad = jnp.einsum(
        "hpk,khd->phd", score_grad, k3.astype(jnp.float32), precision=HIGHEST,
        preferred_element_type=jnp.float32,
    ) * scale
    key_ext_grad = jnp.einsum(
        "hpk,phd->khd", score_grad, q3.astype(jnp.float32), precision=HIGHEST,
        preferred_element_type=jnp.float32,
    ) * scale
    value_ext_grad = jnp.einsum(
        "hpk,phd->khd", probs, ag3.astype(jnp.float32), precision=HIGHEST,
        preferred_element_type=jnp.float32,
    )
    buffer = jnp.concatenate(
        [key_ext_grad.reshape(ext_rows, ext_cols, width), value_ext_grad.reshape(ext_rows, ext_cols, width)],
        axis=-1,
    )
    from_below = passed_along(buffer[:reach], "row", -1)
    from_above = passed_along(buffer[reach + rows :], "row", 1)
    middle = buffer[reach : reach + rows]
    middle = middle.at[:reach].add(from_above)
    middle = middle.at[rows - reach :].add(from_below)
    from_right = passed_along(middle[:, :reach].astype(jnp.bfloat16), "col", -1).astype(jnp.float32)
    from_left = passed_along(middle[:, reach + cols :].astype(jnp.bfloat16), "col", 1).astype(
        jnp.float32
    )
    inner = middle[:, reach : reach + cols]
    inner = inner.at[:, :reach].add(from_left)
    inner = inner.at[:, cols - reach :].add(from_right)
    joined_grad = jnp.concatenate(
        [query_grad.reshape(rows, cols, width), inner], axis=-1
    ).astype(jnp.bfloat16)
    joined_grad = joined_grad.reshape(-1, 3 * width)
    normed_gradient = jnp.dot(joined_grad, full_qkv.T, preferred_element_type=jnp.float32).reshape(
        rows, cols, width
    )
    qkv_term = jnp.dot(flat.T, joined_grad, preferred_element_type=jnp.float32)
    gain_product = jnp.sum(normed_gradient * standardized_input, axis=(0, 1))
    scaled_features = normed_gradient * layer_norm_gain
    patch_gradient = upstream.astype(jnp.float32) + inverse_deviation * (
        scaled_features
        - jnp.mean(scaled_features, axis=-1, keepdims=True)
        - standardized_input
        * jnp.mean(scaled_features * standardized_input, axis=-1, keepdims=True)
    )
    row_count = lax.axis_size("row")
    heads_per, rows_per = heads // row_count, width // row_count
    bias_rows = jnp.pad(
        bias_term.reshape(row_count, heads_per, -1), ((0, 0), (0, rows_per - heads_per), (0, 0))
    ).reshape(width, -1)
    offsets = bias_term.shape[1]
    spare = 128 - 1 - offsets
    extra = jnp.concatenate(
        [gain_product[:, None], bias_rows, jnp.zeros((width, spare), jnp.float32)], axis=1
    ).astype(jnp.bfloat16)
    qkv_sum, extra_sum = lax.psum(
        lax.psum_scatter(
            (qkv_term.astype(jnp.bfloat16), extra), "row", scatter_dimension=0, tiled=True
        ),
        "col",
    )
    qkv_sum = qkv_sum.astype(jnp.float32)
    extra_sum = extra_sum.astype(jnp.float32)
    gain_sum = extra_sum[:, 0]
    bias_sum = extra_sum[:heads_per, 1 : 1 + offsets]
    return (patch_gradient, qkv_sum, out_sum, gain_sum, bias_sum)


def solution(mesh):
    in_specs = (
        P(("grp", "row"), "col", None),
        P(("grp", "row"), "col", None),
        P("row", None),
        P("row", None),
        P(),
        P(),
        P(("grp", "row"), "col"),
    )
    out_specs = (
        P(("grp", "row"), "col", None),
        P(("grp", "row"), None),
        P(("grp", "row"), None),
        P(("grp", "row")),
        P(("grp", "row"), None),
    )
    return jax.shard_map(body, mesh=mesh, in_specs=in_specs, out_specs=out_specs, check_vma=False)
```

```python
import jax
import jax.numpy as jnp
from jax import lax
from jax.sharding import PartitionSpec as P

RAD = 3
HIGHEST = lax.Precision.HIGHEST


def extended_2(shard, sides, width):
    for axis, dim in sides:
        devices, length = (lax.axis_size(axis), shard.shape[dim])
        up = [(i, i + 1) for i in range(devices - 1)]
        down = [(j, i) for i, j in up]
        last = lax.slice_in_dim(shard, length - width, length, axis=dim)
        first = lax.slice_in_dim(shard, 0, width, axis=dim)
        before = lax.ppermute(last, axis, up)
        after = lax.ppermute(first, axis, down)
        shard = jnp.concatenate([before, shard, after], axis=dim)
    return shard


def passed_along(value, axis, steps):
    count = lax.axis_size(axis)
    first, last = (max(0, -steps), min(count, count - steps))
    return lax.ppermute(value, axis, [(source, source + steps) for source in range(first, last)])


def apply_layer_norm(values, norm_gain_value):
    floats = values.astype(jnp.float32)
    feature_mean = jnp.mean(floats, axis=-1, keepdims=True)
    mean_removed = floats - feature_mean
    variance = jnp.mean(mean_removed * mean_removed, axis=-1, keepdims=True)
    inverse_deviation = lax.rsqrt(variance + 1e-05)
    standardized_input = mean_removed * inverse_deviation
    return (
        (standardized_input * norm_gain_value).astype(jnp.bfloat16),
        standardized_input,
        inverse_deviation,
    )


def window_tables(rows, cols, reach):
    side = 2 * reach + 1
    shape = (rows, cols, rows + 2 * reach, cols + 2 * reach)
    row_gap = lax.broadcasted_iota(jnp.int32, shape, 2) - lax.broadcasted_iota(jnp.int32, shape, 0)
    col_gap = lax.broadcasted_iota(jnp.int32, shape, 3) - lax.broadcasted_iota(jnp.int32, shape, 1)
    inside = (row_gap >= 0) & (row_gap < side) & (col_gap >= 0) & (col_gap < side)
    offset_id = jnp.where(inside, row_gap * side + col_gap, -1)
    centre = (row_gap == reach) & (col_gap == reach)
    nq = rows * cols
    nk = (rows + 2 * reach) * (cols + 2 * reach)
    offset_id = offset_id.reshape(nq * nk)
    one_hot = (
        offset_id[None, :] == lax.broadcasted_iota(jnp.int32, (side * side, nq * nk), 0)
    ).astype(jnp.float32)
    return inside.reshape(nq, nk), centre.reshape(nq, nk), one_hot


def body(patches, upstream, qkv_weight, out_weight, layer_norm_gain, pos_bias, valid_mask):
    rows, cols, width = patches.shape
    heads = pos_bias.shape[0]
    hdim = width // heads
    reach = RAD
    ext_rows, ext_cols = rows + 2 * reach, cols + 2 * reach
    nq, nk = rows * cols, ext_rows * ext_cols
    scale = float(hdim) ** (-0.5)
    full_qkv, full_out = (
        lax.all_gather(qkv_weight, "row", axis=0, tiled=True),
        lax.all_gather(out_weight, "row", axis=0, tiled=True),
    )
    normed_features, standardized_input, inverse_deviation = apply_layer_norm(
        patches, layer_norm_gain
    )
    flat = normed_features.reshape(-1, width)
    joined = jnp.dot(flat, full_qkv, preferred_element_type=jnp.float32).astype(jnp.bfloat16)
    query = joined[:, :width]
    kv = joined[:, width:].reshape(rows, cols, 2 * width)
    kv_ext = extended_2(kv, (("row", 0), ("col", 1)), reach).reshape(nk, 2 * width)
    mask_ext = extended_2(valid_mask, (("row", 0), ("col", 1)), reach).reshape(nk)
    q3 = query.reshape(nq, heads, hdim)
    k3 = kv_ext[:, :width].reshape(nk, heads, hdim)
    v3 = kv_ext[:, width:].reshape(nk, heads, hdim)

    inside, centre, one_hot = window_tables(rows, cols, reach)
    allowed = inside & ((mask_ext[None, :] == 1) | centre)
    bias_full = jnp.dot(pos_bias, one_hot, precision=HIGHEST).reshape(heads, nq, nk)
    raw = jnp.einsum("phd,khd->hpk", q3, k3, preferred_element_type=jnp.float32)
    scores = jnp.where(allowed[None], raw * scale + bias_full, -jnp.inf)
    top = jnp.max(scores, axis=-1, keepdims=True)
    expo = jnp.exp(scores - top)
    denom = jnp.sum(expo, axis=-1, keepdims=True)
    probs = expo / denom
    attended3 = jnp.einsum(
        "hpk,khd->phd", probs, v3.astype(jnp.float32), precision=HIGHEST,
        preferred_element_type=jnp.float32,
    )
    attended = attended3.astype(jnp.bfloat16).reshape(nq, width)

    grad_flat = upstream.reshape(-1, width)
    out_grad = jnp.dot(attended.T, grad_flat, preferred_element_type=jnp.float32)
    out_sum = lax.all_gather(
        lax.psum_scatter(out_grad.astype(jnp.bfloat16), ("row", "col"), scatter_dimension=0, tiled=True),
        "col", axis=0, tiled=True,
    ).astype(jnp.float32)
    attended_grad = jnp.dot(grad_flat, full_out.T, preferred_element_type=jnp.float32).astype(
        jnp.bfloat16
    )
    ag3 = attended_grad.reshape(nq, heads, hdim)
    delta = jnp.sum(
        ag3.astype(jnp.float32) * attended.reshape(nq, heads, hdim).astype(jnp.float32), axis=-1
    )
    prob_grad = jnp.einsum("phd,khd->hpk", ag3, v3, preferred_element_type=jnp.float32)
    score_grad = probs * (prob_grad - delta.T[:, :, None])
    bias_term = jnp.dot(
        score_grad.reshape(heads, nq * nk), one_hot.T, precision=HIGHEST,
        preferred_element_type=jnp.float32,
    )
    query_grad = jnp.einsum(
        "hpk,khd->phd", score_grad, k3.astype(jnp.float32), precision=HIGHEST,
        preferred_element_type=jnp.float32,
    ) * scale
    key_ext_grad = jnp.einsum(
        "hpk,phd->khd", score_grad, q3.astype(jnp.float32), precision=HIGHEST,
        preferred_element_type=jnp.float32,
    ) * scale
    value_ext_grad = jnp.einsum(
        "hpk,phd->khd", probs, ag3.astype(jnp.float32), precision=HIGHEST,
        preferred_element_type=jnp.float32,
    )
    buffer = jnp.concatenate(
        [key_ext_grad.reshape(ext_rows, ext_cols, width), value_ext_grad.reshape(ext_rows, ext_cols, width)],
        axis=-1,
    )
    from_below = passed_along(buffer[:reach], "row", -1)
    from_above = passed_along(buffer[reach + rows :], "row", 1)
    middle = buffer[reach : reach + rows]
    middle = middle.at[:reach].add(from_above)
    middle = middle.at[rows - reach :].add(from_below)
    from_right = passed_along(middle[:, :reach].astype(jnp.bfloat16), "col", -1).astype(jnp.float32)
    from_left = passed_along(middle[:, reach + cols :].astype(jnp.bfloat16), "col", 1).astype(
        jnp.float32
    )
    inner = middle[:, reach : reach + cols]
    inner = inner.at[:, :reach].add(from_left)
    inner = inner.at[:, cols - reach :].add(from_right)
    joined_grad = jnp.concatenate(
        [query_grad.reshape(rows, cols, width), inner], axis=-1
    ).astype(jnp.bfloat16)
    joined_grad = joined_grad.reshape(-1, 3 * width)
    normed_gradient = jnp.dot(joined_grad, full_qkv.T, preferred_element_type=jnp.float32).reshape(
        rows, cols, width
    )
    qkv_term = jnp.dot(flat.T, joined_grad, preferred_element_type=jnp.float32)
    gain_product = jnp.sum(normed_gradient * standardized_input, axis=(0, 1))
    scaled_features = normed_gradient * layer_norm_gain
    patch_gradient = upstream.astype(jnp.float32) + inverse_deviation * (
        scaled_features
        - jnp.mean(scaled_features, axis=-1, keepdims=True)
        - standardized_input
        * jnp.mean(scaled_features * standardized_input, axis=-1, keepdims=True)
    )
    row_count = lax.axis_size("row")
    heads_per, rows_per = heads // row_count, width // row_count
    bias_rows = jnp.pad(
        bias_term.reshape(row_count, heads_per, -1), ((0, 0), (0, rows_per - heads_per), (0, 0))
    ).reshape(width, -1)
    offsets = bias_term.shape[1]
    spare = 128 - 1 - offsets
    big = jnp.concatenate(
        [qkv_term, gain_product[:, None], bias_rows, jnp.zeros((width, spare), jnp.float32)], axis=1
    ).astype(jnp.bfloat16)
    big_sum = lax.all_gather(
        lax.psum_scatter(big, ("row", "col"), scatter_dimension=0, tiled=True), "col", axis=0, tiled=True
    )
    big_sum = big_sum.astype(jnp.float32)
    qkv_sum = big_sum[:, : 3 * width]
    gain_sum = big_sum[:, 3 * width]
    bias_sum = big_sum[:heads_per, 3 * width + 1 : 3 * width + 1 + offsets]
    return (patch_gradient, qkv_sum, out_sum, gain_sum, bias_sum)


def solution(mesh):
    in_specs = (
        P(("grp", "row"), "col", None),
        P(("grp", "row"), "col", None),
        P("row", None),
        P("row", None),
        P(),
        P(),
        P(("grp", "row"), "col"),
    )
    out_specs = (
        P(("grp", "row"), "col", None),
        P(("grp", "row"), None),
        P(("grp", "row"), None),
        P(("grp", "row")),
        P(("grp", "row"), None),
    )
    return jax.shard_map(body, mesh=mesh, in_specs=in_specs, out_specs=out_specs, check_vma=False)
```

```python
import jax
import jax.numpy as jnp
from jax import lax
from jax.sharding import PartitionSpec as P

RAD = 3
HIGHEST = lax.Precision.HIGHEST
HIGH = lax.Precision.HIGH


def extended_2(shard, sides, width):
    for axis, dim in sides:
        devices, length = (lax.axis_size(axis), shard.shape[dim])
        up = [(i, i + 1) for i in range(devices - 1)]
        down = [(j, i) for i, j in up]
        last = lax.slice_in_dim(shard, length - width, length, axis=dim)
        first = lax.slice_in_dim(shard, 0, width, axis=dim)
        before = lax.ppermute(last, axis, up)
        after = lax.ppermute(first, axis, down)
        shard = jnp.concatenate([before, shard, after], axis=dim)
    return shard


def passed_along(value, axis, steps):
    count = lax.axis_size(axis)
    first, last = (max(0, -steps), min(count, count - steps))
    return lax.ppermute(value, axis, [(source, source + steps) for source in range(first, last)])


def apply_layer_norm(values, norm_gain_value):
    floats = values.astype(jnp.float32)
    feature_mean = jnp.mean(floats, axis=-1, keepdims=True)
    mean_removed = floats - feature_mean
    variance = jnp.mean(mean_removed * mean_removed, axis=-1, keepdims=True)
    inverse_deviation = lax.rsqrt(variance + 1e-05)
    standardized_input = mean_removed * inverse_deviation
    return (
        (standardized_input * norm_gain_value).astype(jnp.bfloat16),
        standardized_input,
        inverse_deviation,
    )


def window_tables(rows, cols, reach):
    side = 2 * reach + 1
    shape = (rows, cols, rows + 2 * reach, cols + 2 * reach)
    row_gap = lax.broadcasted_iota(jnp.int32, shape, 2) - lax.broadcasted_iota(jnp.int32, shape, 0)
    col_gap = lax.broadcasted_iota(jnp.int32, shape, 3) - lax.broadcasted_iota(jnp.int32, shape, 1)
    inside = (row_gap >= 0) & (row_gap < side) & (col_gap >= 0) & (col_gap < side)
    offset_id = jnp.where(inside, row_gap * side + col_gap, -1)
    centre = (row_gap == reach) & (col_gap == reach)
    nq = rows * cols
    nk = (rows + 2 * reach) * (cols + 2 * reach)
    offset_id = offset_id.reshape(nq * nk)
    one_hot = (
        offset_id[None, :] == lax.broadcasted_iota(jnp.int32, (side * side, nq * nk), 0)
    ).astype(jnp.float32)
    return inside.reshape(nq, nk), centre.reshape(nq, nk), one_hot


def body(patches, upstream, qkv_weight, out_weight, layer_norm_gain, pos_bias, valid_mask):
    rows, cols, width = patches.shape
    heads = pos_bias.shape[0]
    hdim = width // heads
    reach = RAD
    ext_rows, ext_cols = rows + 2 * reach, cols + 2 * reach
    nq, nk = rows * cols, ext_rows * ext_cols
    scale = float(hdim) ** (-0.5)
    full_qkv, full_out = (
        lax.all_gather(qkv_weight, "row", axis=0, tiled=True),
        lax.all_gather(out_weight, "row", axis=0, tiled=True),
    )
    normed_features, standardized_input, inverse_deviation = apply_layer_norm(
        patches, layer_norm_gain
    )
    flat = normed_features.reshape(-1, width)
    joined = jnp.dot(flat, full_qkv, preferred_element_type=jnp.float32).astype(jnp.bfloat16)
    query = joined[:, :width]
    kv = joined[:, width:].reshape(rows, cols, 2 * width)
    kv_ext = extended_2(kv, (("row", 0), ("col", 1)), reach).reshape(nk, 2 * width)
    mask_ext = extended_2(valid_mask, (("row", 0), ("col", 1)), reach).reshape(nk)
    q3 = query.reshape(nq, heads, hdim)
    k3 = kv_ext[:, :width].reshape(nk, heads, hdim)
    v3 = kv_ext[:, width:].reshape(nk, heads, hdim)

    inside, centre, one_hot = window_tables(rows, cols, reach)
    allowed = inside & ((mask_ext[None, :] == 1) | centre)
    bias_full = jnp.dot(pos_bias, one_hot, precision=HIGHEST).reshape(heads, nq, nk)
    raw = jnp.einsum("phd,khd->hpk", q3, k3, preferred_element_type=jnp.float32)
    scores = jnp.where(allowed[None], raw * scale + bias_full, -jnp.inf)
    top = jnp.max(scores, axis=-1, keepdims=True)
    expo = jnp.exp(scores - top)
    denom = jnp.sum(expo, axis=-1, keepdims=True)
    probs = expo / denom
    attended3 = jnp.einsum(
        "hpk,khd->phd", probs, v3.astype(jnp.float32), precision=HIGH,
        preferred_element_type=jnp.float32,
    )
    attended = attended3.astype(jnp.bfloat16).reshape(nq, width)

    grad_flat = upstream.reshape(-1, width)
    out_grad = jnp.dot(attended.T, grad_flat, preferred_element_type=jnp.float32)
    out_sum = lax.psum(
        lax.psum_scatter(out_grad.astype(jnp.bfloat16), "row", scatter_dimension=0, tiled=True), "col"
    ).astype(jnp.float32)
    attended_grad = jnp.dot(grad_flat, full_out.T, preferred_element_type=jnp.float32).astype(
        jnp.bfloat16
    )
    ag3 = attended_grad.reshape(nq, heads, hdim)
    delta = jnp.sum(
        ag3.astype(jnp.float32) * attended.reshape(nq, heads, hdim).astype(jnp.float32), axis=-1
    )
    prob_grad = jnp.einsum("phd,khd->hpk", ag3, v3, preferred_element_type=jnp.float32)
    score_grad = probs * (prob_grad - delta.T[:, :, None])
    bias_term = jnp.dot(
        score_grad.reshape(heads, nq * nk), one_hot.T, precision=HIGH,
        preferred_element_type=jnp.float32,
    )
    query_grad = jnp.einsum(
        "hpk,khd->phd", score_grad, k3.astype(jnp.float32), precision=HIGH,
        preferred_element_type=jnp.float32,
    ) * scale
    key_ext_grad = jnp.einsum(
        "hpk,phd->khd", score_grad, q3.astype(jnp.float32), precision=HIGH,
        preferred_element_type=jnp.float32,
    ) * scale
    value_ext_grad = jnp.einsum(
        "hpk,phd->khd", probs, ag3.astype(jnp.float32), precision=HIGH,
        preferred_element_type=jnp.float32,
    )
    query_term = jnp.dot(
        flat.T, query_grad.reshape(nq, width).astype(jnp.bfloat16), preferred_element_type=jnp.float32
    ).astype(jnp.bfloat16)
    out_sum, query_term = lax.optimization_barrier((out_sum, query_term))
    query_sum = lax.psum(lax.psum_scatter(query_term, "row", scatter_dimension=0, tiled=True), "col")
    buffer = jnp.concatenate(
        [key_ext_grad.reshape(ext_rows, ext_cols, width), value_ext_grad.reshape(ext_rows, ext_cols, width)],
        axis=-1,
    )
    from_below = passed_along(buffer[:reach], "row", -1)
    from_above = passed_along(buffer[reach + rows :], "row", 1)
    middle = buffer[reach : reach + rows]
    middle = middle.at[:reach].add(from_above)
    middle = middle.at[rows - reach :].add(from_below)
    from_right = passed_along(middle[:, :reach].astype(jnp.bfloat16), "col", -1).astype(jnp.float32)
    from_left = passed_along(middle[:, reach + cols :].astype(jnp.bfloat16), "col", 1).astype(
        jnp.float32
    )
    inner = middle[:, reach : reach + cols]
    inner = inner.at[:, :reach].add(from_left)
    inner = inner.at[:, cols - reach :].add(from_right)
    joined_grad = jnp.concatenate(
        [query_grad.reshape(rows, cols, width), inner], axis=-1
    ).astype(jnp.bfloat16)
    joined_grad = joined_grad.reshape(-1, 3 * width)
    normed_gradient = jnp.dot(joined_grad, full_qkv.T, preferred_element_type=jnp.float32).reshape(
        rows, cols, width
    )
    gain_product = jnp.sum(normed_gradient * standardized_input, axis=(0, 1))
    scaled_features = normed_gradient * layer_norm_gain
    patch_gradient = upstream.astype(jnp.float32) + inverse_deviation * (
        scaled_features
        - jnp.mean(scaled_features, axis=-1, keepdims=True)
        - standardized_input
        * jnp.mean(scaled_features * standardized_input, axis=-1, keepdims=True)
    )
    row_count = lax.axis_size("row")
    heads_per, rows_per = heads // row_count, width // row_count
    bias_rows = jnp.pad(
        bias_term.reshape(row_count, heads_per, -1), ((0, 0), (0, rows_per - heads_per), (0, 0))
    ).reshape(width, -1)
    offsets = bias_term.shape[1]
    spare = 128 - 1 - offsets
    kv_pad = jnp.pad(joined_grad[:, width:], ((0, 0), (0, 128)))
    big = jnp.dot(flat.T, kv_pad, preferred_element_type=jnp.float32).astype(jnp.bfloat16)
    extra = jnp.concatenate(
        [gain_product[:, None], bias_rows, jnp.zeros((width, spare), jnp.float32)], axis=1
    ).astype(jnp.bfloat16)
    big = lax.dynamic_update_slice_in_dim(big, extra, 2 * width, axis=1)
    query_sum, big = lax.optimization_barrier((query_sum, big))
    big_sum = lax.psum(lax.psum_scatter(big, "row", scatter_dimension=0, tiled=True), "col")
    big_sum = big_sum.astype(jnp.float32)
    qkv_sum = jnp.concatenate([query_sum.astype(jnp.float32), big_sum[:, : 2 * width]], axis=1)
    gain_sum = big_sum[:, 2 * width]
    bias_sum = big_sum[:heads_per, 2 * width + 1 : 2 * width + 1 + offsets]
    return (patch_gradient, qkv_sum, out_sum, gain_sum, bias_sum)


def solution(mesh):
    in_specs = (
        P(("grp", "row"), "col", None),
        P(("grp", "row"), "col", None),
        P("row", None),
        P("row", None),
        P(),
        P(),
        P(("grp", "row"), "col"),
    )
    out_specs = (
        P(("grp", "row"), "col", None),
        P(("grp", "row"), None),
        P(("grp", "row"), None),
        P(("grp", "row")),
        P(("grp", "row"), None),
    )
    return jax.shard_map(body, mesh=mesh, in_specs=in_specs, out_specs=out_specs, check_vma=False)
```

```python
import jax
import jax.numpy as jnp
from jax import lax
from jax.sharding import PartitionSpec as P

RAD = 3
HIGHEST = lax.Precision.HIGHEST
HIGH = lax.Precision.HIGH


def extended_2(shard, sides, width):
    for axis, dim in sides:
        devices, length = (lax.axis_size(axis), shard.shape[dim])
        up = [(i, i + 1) for i in range(devices - 1)]
        down = [(j, i) for i, j in up]
        last = lax.slice_in_dim(shard, length - width, length, axis=dim)
        first = lax.slice_in_dim(shard, 0, width, axis=dim)
        before = lax.ppermute(last, axis, up)
        after = lax.ppermute(first, axis, down)
        shard = jnp.concatenate([before, shard, after], axis=dim)
    return shard


def passed_along(value, axis, steps):
    count = lax.axis_size(axis)
    first, last = (max(0, -steps), min(count, count - steps))
    return lax.ppermute(value, axis, [(source, source + steps) for source in range(first, last)])


def apply_layer_norm(values, norm_gain_value):
    floats = values.astype(jnp.float32)
    feature_mean = jnp.mean(floats, axis=-1, keepdims=True)
    mean_removed = floats - feature_mean
    variance = jnp.mean(mean_removed * mean_removed, axis=-1, keepdims=True)
    inverse_deviation = lax.rsqrt(variance + 1e-05)
    standardized_input = mean_removed * inverse_deviation
    return (
        (standardized_input * norm_gain_value).astype(jnp.bfloat16),
        standardized_input,
        inverse_deviation,
    )


def window_tables(rows, cols, reach):
    side = 2 * reach + 1
    shape = (rows, cols, rows + 2 * reach, cols + 2 * reach)
    row_gap = lax.broadcasted_iota(jnp.int32, shape, 2) - lax.broadcasted_iota(jnp.int32, shape, 0)
    col_gap = lax.broadcasted_iota(jnp.int32, shape, 3) - lax.broadcasted_iota(jnp.int32, shape, 1)
    inside = (row_gap >= 0) & (row_gap < side) & (col_gap >= 0) & (col_gap < side)
    offset_id = jnp.where(inside, row_gap * side + col_gap, -1)
    centre = (row_gap == reach) & (col_gap == reach)
    nq = rows * cols
    nk = (rows + 2 * reach) * (cols + 2 * reach)
    offset_id = offset_id.reshape(nq * nk)
    one_hot = (
        offset_id[None, :] == lax.broadcasted_iota(jnp.int32, (side * side, nq * nk), 0)
    ).astype(jnp.float32)
    return inside.reshape(nq, nk), centre.reshape(nq, nk), one_hot


def body(patches, upstream, qkv_weight, out_weight, layer_norm_gain, pos_bias, valid_mask):
    rows, cols, width = patches.shape
    heads = pos_bias.shape[0]
    hdim = width // heads
    reach = RAD
    ext_rows, ext_cols = rows + 2 * reach, cols + 2 * reach
    nq, nk = rows * cols, ext_rows * ext_cols
    scale = float(hdim) ** (-0.5)
    full_qkv, full_out = (
        lax.all_gather(qkv_weight, "row", axis=0, tiled=True),
        lax.all_gather(out_weight, "row", axis=0, tiled=True),
    )
    normed_features, standardized_input, inverse_deviation = apply_layer_norm(
        patches, layer_norm_gain
    )
    flat = normed_features.reshape(-1, width)
    joined = jnp.dot(flat, full_qkv, preferred_element_type=jnp.float32).astype(jnp.bfloat16)
    query = joined[:, :width]
    kv = joined[:, width:].reshape(rows, cols, 2 * width)
    kv_ext = extended_2(kv, (("row", 0), ("col", 1)), reach).reshape(nk, 2 * width)
    mask_ext = extended_2(valid_mask, (("row", 0), ("col", 1)), reach).reshape(nk)
    q3 = query.reshape(nq, heads, hdim)
    k3 = kv_ext[:, :width].reshape(nk, heads, hdim)
    v3 = kv_ext[:, width:].reshape(nk, heads, hdim)

    inside, centre, one_hot = window_tables(rows, cols, reach)
    allowed = inside & ((mask_ext[None, :] == 1) | centre)
    bias_full = jnp.dot(pos_bias, one_hot, precision=HIGHEST).reshape(heads, nq, nk)
    raw = jnp.einsum("phd,khd->hpk", q3, k3, preferred_element_type=jnp.float32)
    scores = jnp.where(allowed[None], raw * scale + bias_full, -jnp.inf)
    top = jnp.max(scores, axis=-1, keepdims=True)
    expo = jnp.exp(scores - top)
    denom = jnp.sum(expo, axis=-1, keepdims=True)
    probs = expo / denom
    attended3 = jnp.einsum(
        "hpk,khd->phd", probs, v3.astype(jnp.float32), precision=HIGH,
        preferred_element_type=jnp.float32,
    )
    attended = attended3.astype(jnp.bfloat16).reshape(nq, width)

    grad_flat = upstream.reshape(-1, width)
    out_grad = jnp.dot(attended.T, grad_flat, preferred_element_type=jnp.float32)
    out_sum = lax.psum(
        lax.psum_scatter(out_grad.astype(jnp.bfloat16), "row", scatter_dimension=0, tiled=True), "col"
    ).astype(jnp.float32)
    attended_grad = jnp.dot(grad_flat, full_out.T, preferred_element_type=jnp.float32).astype(
        jnp.bfloat16
    )
    ag3 = attended_grad.reshape(nq, heads, hdim)
    delta = jnp.sum(
        ag3.astype(jnp.float32) * attended.reshape(nq, heads, hdim).astype(jnp.float32), axis=-1
    )
    prob_grad = jnp.einsum("phd,khd->hpk", ag3, v3, preferred_element_type=jnp.float32)
    score_grad = probs * (prob_grad - delta.T[:, :, None])
    bias_term = jnp.dot(
        score_grad.reshape(heads, nq * nk), one_hot.T, precision=HIGH,
        preferred_element_type=jnp.float32,
    )
    query_grad = jnp.einsum(
        "hpk,khd->phd", score_grad, k3.astype(jnp.float32), precision=HIGH,
        preferred_element_type=jnp.float32,
    ) * scale
    key_ext_grad = jnp.einsum(
        "hpk,phd->khd", score_grad, q3.astype(jnp.float32), precision=HIGH,
        preferred_element_type=jnp.float32,
    ) * scale
    value_ext_grad = jnp.einsum(
        "hpk,phd->khd", probs, ag3.astype(jnp.float32), precision=HIGH,
        preferred_element_type=jnp.float32,
    )
    buffer = jnp.concatenate(
        [key_ext_grad.reshape(ext_rows, ext_cols, width), value_ext_grad.reshape(ext_rows, ext_cols, width)],
        axis=-1,
    )
    from_below = passed_along(buffer[:reach], "row", -1)
    from_above = passed_along(buffer[reach + rows :], "row", 1)
    middle = buffer[reach : reach + rows]
    middle = middle.at[:reach].add(from_above)
    middle = middle.at[rows - reach :].add(from_below)
    from_right = passed_along(middle[:, :reach].astype(jnp.bfloat16), "col", -1).astype(jnp.float32)
    from_left = passed_along(middle[:, reach + cols :].astype(jnp.bfloat16), "col", 1).astype(
        jnp.float32
    )
    inner = middle[:, reach : reach + cols]
    inner = inner.at[:, :reach].add(from_left)
    inner = inner.at[:, cols - reach :].add(from_right)
    joined_grad = jnp.concatenate(
        [query_grad.reshape(rows, cols, width), inner], axis=-1
    ).astype(jnp.bfloat16)
    joined_grad = joined_grad.reshape(-1, 3 * width)
    normed_gradient = jnp.dot(joined_grad, full_qkv.T, preferred_element_type=jnp.float32).reshape(
        rows, cols, width
    )
    gain_product = jnp.sum(normed_gradient * standardized_input, axis=(0, 1))
    scaled_features = normed_gradient * layer_norm_gain
    patch_gradient = upstream.astype(jnp.float32) + inverse_deviation * (
        scaled_features
        - jnp.mean(scaled_features, axis=-1, keepdims=True)
        - standardized_input
        * jnp.mean(scaled_features * standardized_input, axis=-1, keepdims=True)
    )
    row_count = lax.axis_size("row")
    heads_per, rows_per = heads // row_count, width // row_count
    bias_rows = jnp.pad(
        bias_term.reshape(row_count, heads_per, -1), ((0, 0), (0, rows_per - heads_per), (0, 0))
    ).reshape(width, -1)
    offsets = bias_term.shape[1]
    spare = 128 - 1 - offsets
    joined_pad = jnp.pad(joined_grad, ((0, 0), (0, 128)))
    big = jnp.dot(flat.T, joined_pad, preferred_element_type=jnp.float32).astype(jnp.bfloat16)
    extra = jnp.concatenate(
        [gain_product[:, None], bias_rows, jnp.zeros((width, spare), jnp.float32)], axis=1
    ).astype(jnp.bfloat16)
    big = lax.dynamic_update_slice_in_dim(big, extra, 3 * width, axis=1)
    big_sum = lax.psum(lax.psum_scatter(big, "row", scatter_dimension=0, tiled=True), "col")
    big_sum = big_sum.astype(jnp.float32)
    qkv_sum = big_sum[:, : 3 * width]
    gain_sum = big_sum[:, 3 * width]
    bias_sum = big_sum[:heads_per, 3 * width + 1 : 3 * width + 1 + offsets]
    return (patch_gradient, qkv_sum, out_sum, gain_sum, bias_sum)


def solution(mesh):
    in_specs = (
        P(("grp", "row"), "col", None),
        P(("grp", "row"), "col", None),
        P("row", None),
        P("row", None),
        P(),
        P(),
        P(("grp", "row"), "col"),
    )
    out_specs = (
        P(("grp", "row"), "col", None),
        P(("grp", "row"), None),
        P(("grp", "row"), None),
        P(("grp", "row")),
        P(("grp", "row"), None),
    )
    return jax.shard_map(body, mesh=mesh, in_specs=in_specs, out_specs=out_specs, check_vma=False)
```

```python
import jax
import jax.numpy as jnp
from jax import lax
from jax.sharding import PartitionSpec as P

RAD = 3
HIGHEST = lax.Precision.HIGHEST
HIGH = lax.Precision.HIGH


def extended_2(shard, sides, width):
    for axis, dim in sides:
        devices, length = (lax.axis_size(axis), shard.shape[dim])
        up = [(i, i + 1) for i in range(devices - 1)]
        down = [(j, i) for i, j in up]
        last = lax.slice_in_dim(shard, length - width, length, axis=dim)
        first = lax.slice_in_dim(shard, 0, width, axis=dim)
        before = lax.ppermute(last, axis, up)
        after = lax.ppermute(first, axis, down)
        shard = jnp.concatenate([before, shard, after], axis=dim)
    return shard


def passed_along(value, axis, steps):
    count = lax.axis_size(axis)
    first, last = (max(0, -steps), min(count, count - steps))
    return lax.ppermute(value, axis, [(source, source + steps) for source in range(first, last)])


def col_all_reduce(value):
    part = lax.psum_scatter(lax.optimization_barrier(value), "col", scatter_dimension=0, tiled=True)
    return lax.all_gather(part, "col", axis=0, tiled=True)


def apply_layer_norm(values, norm_gain_value):
    floats = values.astype(jnp.float32)
    feature_mean = jnp.mean(floats, axis=-1, keepdims=True)
    mean_removed = floats - feature_mean
    variance = jnp.mean(mean_removed * mean_removed, axis=-1, keepdims=True)
    inverse_deviation = lax.rsqrt(variance + 1e-05)
    standardized_input = mean_removed * inverse_deviation
    return (
        (standardized_input * norm_gain_value).astype(jnp.bfloat16),
        standardized_input,
        inverse_deviation,
    )


def window_tables(rows, cols, reach):
    side = 2 * reach + 1
    shape = (rows, cols, rows + 2 * reach, cols + 2 * reach)
    row_gap = lax.broadcasted_iota(jnp.int32, shape, 2) - lax.broadcasted_iota(jnp.int32, shape, 0)
    col_gap = lax.broadcasted_iota(jnp.int32, shape, 3) - lax.broadcasted_iota(jnp.int32, shape, 1)
    inside = (row_gap >= 0) & (row_gap < side) & (col_gap >= 0) & (col_gap < side)
    offset_id = jnp.where(inside, row_gap * side + col_gap, -1)
    centre = (row_gap == reach) & (col_gap == reach)
    nq = rows * cols
    nk = (rows + 2 * reach) * (cols + 2 * reach)
    offset_id = offset_id.reshape(nq * nk)
    one_hot = (
        offset_id[None, :] == lax.broadcasted_iota(jnp.int32, (side * side, nq * nk), 0)
    ).astype(jnp.float32)
    return inside.reshape(nq, nk), centre.reshape(nq, nk), one_hot


def body(patches, upstream, qkv_weight, out_weight, layer_norm_gain, pos_bias, valid_mask):
    rows, cols, width = patches.shape
    heads = pos_bias.shape[0]
    hdim = width // heads
    reach = RAD
    ext_rows, ext_cols = rows + 2 * reach, cols + 2 * reach
    nq, nk = rows * cols, ext_rows * ext_cols
    scale = float(hdim) ** (-0.5)
    full_qkv, full_out = (
        lax.all_gather(qkv_weight, "row", axis=0, tiled=True),
        lax.all_gather(out_weight, "row", axis=0, tiled=True),
    )
    normed_features, standardized_input, inverse_deviation = apply_layer_norm(
        patches, layer_norm_gain
    )
    flat = normed_features.reshape(-1, width)
    joined = jnp.dot(flat, full_qkv, preferred_element_type=jnp.float32).astype(jnp.bfloat16)
    query = joined[:, :width]
    kv = joined[:, width:].reshape(rows, cols, 2 * width)
    kv_ext = extended_2(kv, (("row", 0), ("col", 1)), reach).reshape(nk, 2 * width)
    mask_ext = extended_2(valid_mask, (("row", 0), ("col", 1)), reach).reshape(nk)
    q3 = query.reshape(nq, heads, hdim)
    k3 = kv_ext[:, :width].reshape(nk, heads, hdim)
    v3 = kv_ext[:, width:].reshape(nk, heads, hdim)

    inside, centre, one_hot = window_tables(rows, cols, reach)
    allowed = inside & ((mask_ext[None, :] == 1) | centre)
    bias_full = jnp.dot(pos_bias, one_hot, precision=HIGHEST).reshape(heads, nq, nk)
    raw = jnp.einsum("phd,khd->hpk", q3, k3, preferred_element_type=jnp.float32)
    scores = jnp.where(allowed[None], raw * scale + bias_full, -jnp.inf)
    top = jnp.max(scores, axis=-1, keepdims=True)
    expo = jnp.exp(scores - top)
    denom = jnp.sum(expo, axis=-1, keepdims=True)
    probs = expo / denom
    attended3 = jnp.einsum(
        "hpk,khd->phd", probs, v3.astype(jnp.float32), precision=HIGH,
        preferred_element_type=jnp.float32,
    )
    attended = attended3.astype(jnp.bfloat16).reshape(nq, width)

    grad_flat = upstream.reshape(-1, width)
    out_grad = jnp.dot(attended.T, grad_flat, preferred_element_type=jnp.float32)
    out_sum = col_all_reduce(
        lax.psum_scatter(out_grad.astype(jnp.bfloat16), "row", scatter_dimension=0, tiled=True)
    ).astype(jnp.float32)
    attended_grad = jnp.dot(grad_flat, full_out.T, preferred_element_type=jnp.float32).astype(
        jnp.bfloat16
    )
    ag3 = attended_grad.reshape(nq, heads, hdim)
    delta = jnp.sum(
        ag3.astype(jnp.float32) * attended.reshape(nq, heads, hdim).astype(jnp.float32), axis=-1
    )
    prob_grad = jnp.einsum("phd,khd->hpk", ag3, v3, preferred_element_type=jnp.float32)
    score_grad = probs * (prob_grad - delta.T[:, :, None])
    bias_term = jnp.dot(
        score_grad.reshape(heads, nq * nk), one_hot.T, precision=HIGH,
        preferred_element_type=jnp.float32,
    )
    query_grad = jnp.einsum(
        "hpk,khd->phd", score_grad, k3.astype(jnp.float32), precision=HIGH,
        preferred_element_type=jnp.float32,
    ) * scale
    key_ext_grad = jnp.einsum(
        "hpk,phd->khd", score_grad, q3.astype(jnp.float32), precision=HIGH,
        preferred_element_type=jnp.float32,
    ) * scale
    value_ext_grad = jnp.einsum(
        "hpk,phd->khd", probs, ag3.astype(jnp.float32), precision=HIGH,
        preferred_element_type=jnp.float32,
    )
    buffer = jnp.concatenate(
        [key_ext_grad.reshape(ext_rows, ext_cols, width), value_ext_grad.reshape(ext_rows, ext_cols, width)],
        axis=-1,
    )
    from_below = passed_along(buffer[:reach], "row", -1)
    from_above = passed_along(buffer[reach + rows :], "row", 1)
    middle = buffer[reach : reach + rows]
    middle = middle.at[:reach].add(from_above)
    middle = middle.at[rows - reach :].add(from_below)
    from_right = passed_along(middle[:, :reach].astype(jnp.bfloat16), "col", -1).astype(jnp.float32)
    from_left = passed_along(middle[:, reach + cols :].astype(jnp.bfloat16), "col", 1).astype(
        jnp.float32
    )
    inner = middle[:, reach : reach + cols]
    inner = inner.at[:, :reach].add(from_left)
    inner = inner.at[:, cols - reach :].add(from_right)
    joined_grad = jnp.concatenate(
        [query_grad.reshape(rows, cols, width), inner], axis=-1
    ).astype(jnp.bfloat16)
    joined_grad = joined_grad.reshape(-1, 3 * width)
    normed_gradient = jnp.dot(joined_grad, full_qkv.T, preferred_element_type=jnp.float32).reshape(
        rows, cols, width
    )
    gain_product = jnp.sum(normed_gradient * standardized_input, axis=(0, 1))
    scaled_features = normed_gradient * layer_norm_gain
    patch_gradient = upstream.astype(jnp.float32) + inverse_deviation * (
        scaled_features
        - jnp.mean(scaled_features, axis=-1, keepdims=True)
        - standardized_input
        * jnp.mean(scaled_features * standardized_input, axis=-1, keepdims=True)
    )
    row_count = lax.axis_size("row")
    heads_per, rows_per = heads // row_count, width // row_count
    bias_rows = jnp.pad(
        bias_term.reshape(row_count, heads_per, -1), ((0, 0), (0, rows_per - heads_per), (0, 0))
    ).reshape(width, -1)
    offsets = bias_term.shape[1]
    spare = 128 - 1 - offsets
    joined_pad = jnp.pad(joined_grad, ((0, 0), (0, 128)))
    big = jnp.dot(flat.T, joined_pad, preferred_element_type=jnp.float32).astype(jnp.bfloat16)
    extra = jnp.concatenate(
        [gain_product[:, None], bias_rows, jnp.zeros((width, spare), jnp.float32)], axis=1
    ).astype(jnp.bfloat16)
    big = lax.dynamic_update_slice_in_dim(big, extra, 3 * width, axis=1)
    big_sum = col_all_reduce(lax.psum_scatter(big, "row", scatter_dimension=0, tiled=True))
    big_sum = big_sum.astype(jnp.float32)
    qkv_sum = big_sum[:, : 3 * width]
    gain_sum = big_sum[:, 3 * width]
    bias_sum = big_sum[:heads_per, 3 * width + 1 : 3 * width + 1 + offsets]
    return (patch_gradient, qkv_sum, out_sum, gain_sum, bias_sum)


def solution(mesh):
    in_specs = (
        P(("grp", "row"), "col", None),
        P(("grp", "row"), "col", None),
        P("row", None),
        P("row", None),
        P(),
        P(),
        P(("grp", "row"), "col"),
    )
    out_specs = (
        P(("grp", "row"), "col", None),
        P(("grp", "row"), None),
        P(("grp", "row"), None),
        P(("grp", "row")),
        P(("grp", "row"), None),
    )
    return jax.shard_map(body, mesh=mesh, in_specs=in_specs, out_specs=out_specs, check_vma=False)
```

```python
import jax
import jax.numpy as jnp
from jax import lax
from jax.sharding import PartitionSpec as P

RAD = 3
HIGHEST = lax.Precision.HIGHEST
HIGH = lax.Precision.HIGH


def extended_2(shard, sides, width):
    for axis, dim in sides:
        devices, length = (lax.axis_size(axis), shard.shape[dim])
        up = [(i, i + 1) for i in range(devices - 1)]
        down = [(j, i) for i, j in up]
        last = lax.slice_in_dim(shard, length - width, length, axis=dim)
        first = lax.slice_in_dim(shard, 0, width, axis=dim)
        before = lax.ppermute(last, axis, up)
        after = lax.ppermute(first, axis, down)
        shard = jnp.concatenate([before, shard, after], axis=dim)
    return shard


def passed_along(value, axis, steps):
    count = lax.axis_size(axis)
    first, last = (max(0, -steps), min(count, count - steps))
    return lax.ppermute(value, axis, [(source, source + steps) for source in range(first, last)])


def apply_layer_norm(values, norm_gain_value):
    floats = values.astype(jnp.float32)
    feature_mean = jnp.mean(floats, axis=-1, keepdims=True)
    mean_removed = floats - feature_mean
    variance = jnp.mean(mean_removed * mean_removed, axis=-1, keepdims=True)
    inverse_deviation = lax.rsqrt(variance + 1e-05)
    standardized_input = mean_removed * inverse_deviation
    return (
        (standardized_input * norm_gain_value).astype(jnp.bfloat16),
        standardized_input,
        inverse_deviation,
    )


def window_tables(rows, cols, reach):
    side = 2 * reach + 1
    shape = (rows, cols, rows + 2 * reach, cols + 2 * reach)
    row_gap = lax.broadcasted_iota(jnp.int32, shape, 2) - lax.broadcasted_iota(jnp.int32, shape, 0)
    col_gap = lax.broadcasted_iota(jnp.int32, shape, 3) - lax.broadcasted_iota(jnp.int32, shape, 1)
    inside = (row_gap >= 0) & (row_gap < side) & (col_gap >= 0) & (col_gap < side)
    offset_id = jnp.where(inside, row_gap * side + col_gap, -1)
    centre = (row_gap == reach) & (col_gap == reach)
    nq = rows * cols
    nk = (rows + 2 * reach) * (cols + 2 * reach)
    offset_id = offset_id.reshape(nq * nk)
    one_hot = (
        offset_id[None, :] == lax.broadcasted_iota(jnp.int32, (side * side, nq * nk), 0)
    ).astype(jnp.float32)
    return inside.reshape(nq, nk), centre.reshape(nq, nk), one_hot


def body(patches, upstream, qkv_weight, out_weight, layer_norm_gain, pos_bias, valid_mask):
    rows, cols, width = patches.shape
    heads = pos_bias.shape[0]
    hdim = width // heads
    reach = RAD
    ext_rows, ext_cols = rows + 2 * reach, cols + 2 * reach
    nq, nk = rows * cols, ext_rows * ext_cols
    scale = float(hdim) ** (-0.5)
    full_qkv, full_out = (
        lax.all_gather(qkv_weight, "row", axis=0, tiled=True),
        lax.all_gather(out_weight, "row", axis=0, tiled=True),
    )
    normed_features, standardized_input, inverse_deviation = apply_layer_norm(
        patches, layer_norm_gain
    )
    flat = normed_features.reshape(-1, width)
    joined = jnp.dot(flat, full_qkv, preferred_element_type=jnp.float32).astype(jnp.bfloat16)
    query = joined[:, :width]
    flags = jnp.broadcast_to(valid_mask.astype(jnp.bfloat16)[:, :, None], (rows, cols, 128))
    kv = jnp.concatenate([joined[:, width:].reshape(rows, cols, 2 * width), flags], axis=-1)
    kv_ext = extended_2(kv, (("row", 0), ("col", 1)), reach).reshape(nk, 2 * width + 128)
    mask_ext = kv_ext[:, 2 * width]
    q3 = query.reshape(nq, heads, hdim)
    k3 = kv_ext[:, :width].reshape(nk, heads, hdim)
    v3 = kv_ext[:, width : 2 * width].reshape(nk, heads, hdim)

    inside, centre, one_hot = window_tables(rows, cols, reach)
    allowed = inside & ((mask_ext[None, :] == 1.0) | centre)
    bias_full = jnp.dot(pos_bias, one_hot, precision=HIGHEST).reshape(heads, nq, nk)
    raw = jnp.einsum("phd,khd->hpk", q3, k3, preferred_element_type=jnp.float32)
    scores = jnp.where(allowed[None], raw * scale + bias_full, -jnp.inf)
    top = jnp.max(scores, axis=-1, keepdims=True)
    expo = jnp.exp(scores - top)
    denom = jnp.sum(expo, axis=-1, keepdims=True)
    probs = expo / denom
    attended3 = jnp.einsum(
        "hpk,khd->phd", probs, v3.astype(jnp.float32), precision=HIGH,
        preferred_element_type=jnp.float32,
    )
    attended = attended3.astype(jnp.bfloat16).reshape(nq, width)

    grad_flat = upstream.reshape(-1, width)
    out_grad = jnp.dot(attended.T, grad_flat, preferred_element_type=jnp.float32)
    out_sum = lax.psum(
        lax.psum_scatter(out_grad.astype(jnp.bfloat16), "row", scatter_dimension=0, tiled=True), "col"
    ).astype(jnp.float32)
    attended_grad = jnp.dot(grad_flat, full_out.T, preferred_element_type=jnp.float32).astype(
        jnp.bfloat16
    )
    ag3 = attended_grad.reshape(nq, heads, hdim)
    delta = jnp.sum(
        ag3.astype(jnp.float32) * attended.reshape(nq, heads, hdim).astype(jnp.float32), axis=-1
    )
    prob_grad = jnp.einsum("phd,khd->hpk", ag3, v3, preferred_element_type=jnp.float32)
    score_grad = probs * (prob_grad - delta.T[:, :, None])
    bias_term = jnp.dot(
        score_grad.reshape(heads, nq * nk), one_hot.T, precision=HIGH,
        preferred_element_type=jnp.float32,
    )
    query_grad = jnp.einsum(
        "hpk,khd->phd", score_grad, k3.astype(jnp.float32), precision=HIGH,
        preferred_element_type=jnp.float32,
    ) * scale
    key_ext_grad = jnp.einsum(
        "hpk,phd->khd", score_grad, q3.astype(jnp.float32), precision=HIGH,
        preferred_element_type=jnp.float32,
    ) * scale
    value_ext_grad = jnp.einsum(
        "hpk,phd->khd", probs, ag3.astype(jnp.float32), precision=HIGH,
        preferred_element_type=jnp.float32,
    )
    buffer = jnp.concatenate(
        [key_ext_grad.reshape(ext_rows, ext_cols, width), value_ext_grad.reshape(ext_rows, ext_cols, width)],
        axis=-1,
    )
    from_below = passed_along(buffer[:reach], "row", -1)
    from_above = passed_along(buffer[reach + rows :], "row", 1)
    middle = buffer[reach : reach + rows]
    middle = middle.at[:reach].add(from_above)
    middle = middle.at[rows - reach :].add(from_below)
    from_right = passed_along(middle[:, :reach].astype(jnp.bfloat16), "col", -1).astype(jnp.float32)
    from_left = passed_along(middle[:, reach + cols :].astype(jnp.bfloat16), "col", 1).astype(
        jnp.float32
    )
    inner = middle[:, reach : reach + cols]
    inner = inner.at[:, :reach].add(from_left)
    inner = inner.at[:, cols - reach :].add(from_right)
    joined_grad = jnp.concatenate(
        [query_grad.reshape(rows, cols, width), inner], axis=-1
    ).astype(jnp.bfloat16)
    joined_grad = joined_grad.reshape(-1, 3 * width)
    normed_gradient = jnp.dot(joined_grad, full_qkv.T, preferred_element_type=jnp.float32).reshape(
        rows, cols, width
    )
    gain_product = jnp.sum(normed_gradient * standardized_input, axis=(0, 1))
    scaled_features = normed_gradient * layer_norm_gain
    patch_gradient = upstream.astype(jnp.float32) + inverse_deviation * (
        scaled_features
        - jnp.mean(scaled_features, axis=-1, keepdims=True)
        - standardized_input
        * jnp.mean(scaled_features * standardized_input, axis=-1, keepdims=True)
    )
    row_count = lax.axis_size("row")
    heads_per, rows_per = heads // row_count, width // row_count
    bias_rows = jnp.pad(
        bias_term.reshape(row_count, heads_per, -1), ((0, 0), (0, rows_per - heads_per), (0, 0))
    ).reshape(width, -1)
    offsets = bias_term.shape[1]
    spare = 128 - 1 - offsets
    joined_pad = jnp.pad(joined_grad, ((0, 0), (0, 128)))
    big = jnp.dot(flat.T, joined_pad, preferred_element_type=jnp.float32).astype(jnp.bfloat16)
    extra = jnp.concatenate(
        [gain_product[:, None], bias_rows, jnp.zeros((width, spare), jnp.float32)], axis=1
    ).astype(jnp.bfloat16)
    big = lax.dynamic_update_slice_in_dim(big, extra, 3 * width, axis=1)
    big_sum = lax.psum(lax.psum_scatter(big, "row", scatter_dimension=0, tiled=True), "col")
    big_sum = big_sum.astype(jnp.float32)
    qkv_sum = big_sum[:, : 3 * width]
    gain_sum = big_sum[:, 3 * width]
    bias_sum = big_sum[:heads_per, 3 * width + 1 : 3 * width + 1 + offsets]
    return (patch_gradient, qkv_sum, out_sum, gain_sum, bias_sum)


def solution(mesh):
    in_specs = (
        P(("grp", "row"), "col", None),
        P(("grp", "row"), "col", None),
        P("row", None),
        P("row", None),
        P(),
        P(),
        P(("grp", "row"), "col"),
    )
    out_specs = (
        P(("grp", "row"), "col", None),
        P(("grp", "row"), None),
        P(("grp", "row"), None),
        P(("grp", "row")),
        P(("grp", "row"), None),
    )
    return jax.shard_map(body, mesh=mesh, in_specs=in_specs, out_specs=out_specs, check_vma=False)
```

```python
import jax
import jax.numpy as jnp
from jax import lax
from jax.sharding import PartitionSpec as P

RAD = 3
HIGHEST = lax.Precision.HIGHEST
HIGH = lax.Precision.HIGH


def extended_2(shard, sides, width):
    for axis, dim in sides:
        devices, length = (lax.axis_size(axis), shard.shape[dim])
        up = [(i, i + 1) for i in range(devices - 1)]
        down = [(j, i) for i, j in up]
        last = lax.slice_in_dim(shard, length - width, length, axis=dim)
        first = lax.slice_in_dim(shard, 0, width, axis=dim)
        before = lax.ppermute(last, axis, up)
        after = lax.ppermute(first, axis, down)
        shard = jnp.concatenate([before, shard, after], axis=dim)
    return shard


def passed_along(value, axis, steps):
    count = lax.axis_size(axis)
    first, last = (max(0, -steps), min(count, count - steps))
    return lax.ppermute(value, axis, [(source, source + steps) for source in range(first, last)])


def gathered_rows(shards):
    count = lax.axis_size("row")
    index = lax.axis_index("row")
    held = [(shards, index)]
    for step in range(2, count, 2):
        pairs = [(r, (r + step) % count) for r in range(count)]
        held.append((lax.ppermute(shards, "row", pairs), (index - step) % count))
    partner = [(r, r ^ 1) for r in range(count)]
    pieces, blocks = [p for p, _ in held], [b for _, b in held]
    swapped = lax.ppermute(tuple(pieces), "row", partner)
    held = held + [(piece, (b ^ 1)) for piece, b in zip(swapped, blocks)]
    outs = []
    for leaf in range(len(shards)):
        size = shards[leaf].shape[0]
        full = jnp.zeros((size * count,) + shards[leaf].shape[1:], shards[leaf].dtype)
        for piece, block in held:
            full = lax.dynamic_update_slice_in_dim(full, piece[leaf], block * size, axis=0)
        outs.append(full)
    return outs


def apply_layer_norm(values, norm_gain_value):
    floats = values.astype(jnp.float32)
    feature_mean = jnp.mean(floats, axis=-1, keepdims=True)
    mean_removed = floats - feature_mean
    variance = jnp.mean(mean_removed * mean_removed, axis=-1, keepdims=True)
    inverse_deviation = lax.rsqrt(variance + 1e-05)
    standardized_input = mean_removed * inverse_deviation
    return (
        (standardized_input * norm_gain_value).astype(jnp.bfloat16),
        standardized_input,
        inverse_deviation,
    )


def window_tables(rows, cols, reach):
    side = 2 * reach + 1
    shape = (rows, cols, rows + 2 * reach, cols + 2 * reach)
    row_gap = lax.broadcasted_iota(jnp.int32, shape, 2) - lax.broadcasted_iota(jnp.int32, shape, 0)
    col_gap = lax.broadcasted_iota(jnp.int32, shape, 3) - lax.broadcasted_iota(jnp.int32, shape, 1)
    inside = (row_gap >= 0) & (row_gap < side) & (col_gap >= 0) & (col_gap < side)
    offset_id = jnp.where(inside, row_gap * side + col_gap, -1)
    centre = (row_gap == reach) & (col_gap == reach)
    nq = rows * cols
    nk = (rows + 2 * reach) * (cols + 2 * reach)
    offset_id = offset_id.reshape(nq * nk)
    one_hot = (
        offset_id[None, :] == lax.broadcasted_iota(jnp.int32, (side * side, nq * nk), 0)
    ).astype(jnp.float32)
    return inside.reshape(nq, nk), centre.reshape(nq, nk), one_hot


def body(patches, upstream, qkv_weight, out_weight, layer_norm_gain, pos_bias, valid_mask):
    rows, cols, width = patches.shape
    heads = pos_bias.shape[0]
    hdim = width // heads
    reach = RAD
    ext_rows, ext_cols = rows + 2 * reach, cols + 2 * reach
    nq, nk = rows * cols, ext_rows * ext_cols
    scale = float(hdim) ** (-0.5)
    full_qkv, full_out = gathered_rows((qkv_weight, out_weight))
    normed_features, standardized_input, inverse_deviation = apply_layer_norm(
        patches, layer_norm_gain
    )
    flat = normed_features.reshape(-1, width)
    joined = jnp.dot(flat, full_qkv, preferred_element_type=jnp.float32).astype(jnp.bfloat16)
    query = joined[:, :width]
    flags = jnp.broadcast_to(valid_mask.astype(jnp.bfloat16)[:, :, None], (rows, cols, 128))
    kv = jnp.concatenate([joined[:, width:].reshape(rows, cols, 2 * width), flags], axis=-1)
    kv_ext = extended_2(kv, (("row", 0), ("col", 1)), reach).reshape(nk, 2 * width + 128)
    mask_ext = kv_ext[:, 2 * width]
    q3 = query.reshape(nq, heads, hdim)
    k3 = kv_ext[:, :width].reshape(nk, heads, hdim)
    v3 = kv_ext[:, width : 2 * width].reshape(nk, heads, hdim)

    inside, centre, one_hot = window_tables(rows, cols, reach)
    allowed = inside & ((mask_ext[None, :] == 1.0) | centre)
    bias_full = jnp.dot(pos_bias, one_hot, precision=HIGHEST).reshape(heads, nq, nk)
    raw = jnp.einsum("phd,khd->hpk", q3, k3, preferred_element_type=jnp.float32)
    scores = jnp.where(allowed[None], raw * scale + bias_full, -jnp.inf)
    top = jnp.max(scores, axis=-1, keepdims=True)
    expo = jnp.exp(scores - top)
    denom = jnp.sum(expo, axis=-1, keepdims=True)
    probs = expo / denom
    attended3 = jnp.einsum(
        "hpk,khd->phd", probs, v3.astype(jnp.float32), precision=HIGH,
        preferred_element_type=jnp.float32,
    )
    attended = attended3.astype(jnp.bfloat16).reshape(nq, width)

    grad_flat = upstream.reshape(-1, width)
    out_grad = jnp.dot(attended.T, grad_flat, preferred_element_type=jnp.float32)
    out_sum = lax.psum(
        lax.psum_scatter(out_grad.astype(jnp.bfloat16), "row", scatter_dimension=0, tiled=True), "col"
    ).astype(jnp.float32)
    attended_grad = jnp.dot(grad_flat, full_out.T, preferred_element_type=jnp.float32).astype(
        jnp.bfloat16
    )
    ag3 = attended_grad.reshape(nq, heads, hdim)
    delta = jnp.sum(
        ag3.astype(jnp.float32) * attended.reshape(nq, heads, hdim).astype(jnp.float32), axis=-1
    )
    prob_grad = jnp.einsum("phd,khd->hpk", ag3, v3, preferred_element_type=jnp.float32)
    score_grad = probs * (prob_grad - delta.T[:, :, None])
    bias_term = jnp.dot(
        score_grad.reshape(heads, nq * nk), one_hot.T, precision=HIGH,
        preferred_element_type=jnp.float32,
    )
    query_grad = jnp.einsum(
        "hpk,khd->phd", score_grad, k3.astype(jnp.float32), precision=HIGH,
        preferred_element_type=jnp.float32,
    ) * scale
    key_ext_grad = jnp.einsum(
        "hpk,phd->khd", score_grad, q3.astype(jnp.float32), precision=HIGH,
        preferred_element_type=jnp.float32,
    ) * scale
    value_ext_grad = jnp.einsum(
        "hpk,phd->khd", probs, ag3.astype(jnp.float32), precision=HIGH,
        preferred_element_type=jnp.float32,
    )
    buffer = jnp.concatenate(
        [key_ext_grad.reshape(ext_rows, ext_cols, width), value_ext_grad.reshape(ext_rows, ext_cols, width)],
        axis=-1,
    )
    from_below = passed_along(buffer[:reach], "row", -1)
    from_above = passed_along(buffer[reach + rows :], "row", 1)
    middle = buffer[reach : reach + rows]
    middle = middle.at[:reach].add(from_above)
    middle = middle.at[rows - reach :].add(from_below)
    from_right = passed_along(middle[:, :reach].astype(jnp.bfloat16), "col", -1).astype(jnp.float32)
    from_left = passed_along(middle[:, reach + cols :].astype(jnp.bfloat16), "col", 1).astype(
        jnp.float32
    )
    inner = middle[:, reach : reach + cols]
    inner = inner.at[:, :reach].add(from_left)
    inner = inner.at[:, cols - reach :].add(from_right)
    joined_grad = jnp.concatenate(
        [query_grad.reshape(rows, cols, width), inner], axis=-1
    ).astype(jnp.bfloat16)
    joined_grad = joined_grad.reshape(-1, 3 * width)
    normed_gradient = jnp.dot(joined_grad, full_qkv.T, preferred_element_type=jnp.float32).reshape(
        rows, cols, width
    )
    gain_product = jnp.sum(normed_gradient * standardized_input, axis=(0, 1))
    scaled_features = normed_gradient * layer_norm_gain
    patch_gradient = upstream.astype(jnp.float32) + inverse_deviation * (
        scaled_features
        - jnp.mean(scaled_features, axis=-1, keepdims=True)
        - standardized_input
        * jnp.mean(scaled_features * standardized_input, axis=-1, keepdims=True)
    )
    row_count = lax.axis_size("row")
    heads_per, rows_per = heads // row_count, width // row_count
    bias_rows = jnp.pad(
        bias_term.reshape(row_count, heads_per, -1), ((0, 0), (0, rows_per - heads_per), (0, 0))
    ).reshape(width, -1)
    offsets = bias_term.shape[1]
    spare = 128 - 1 - offsets
    joined_pad = jnp.pad(joined_grad, ((0, 0), (0, 128)))
    big = jnp.dot(flat.T, joined_pad, preferred_element_type=jnp.float32).astype(jnp.bfloat16)
    extra = jnp.concatenate(
        [gain_product[:, None], bias_rows, jnp.zeros((width, spare), jnp.float32)], axis=1
    ).astype(jnp.bfloat16)
    big = lax.dynamic_update_slice_in_dim(big, extra, 3 * width, axis=1)
    big_sum = lax.psum(lax.psum_scatter(big, "row", scatter_dimension=0, tiled=True), "col")
    big_sum = big_sum.astype(jnp.float32)
    qkv_sum = big_sum[:, : 3 * width]
    gain_sum = big_sum[:, 3 * width]
    bias_sum = big_sum[:heads_per, 3 * width + 1 : 3 * width + 1 + offsets]
    return (patch_gradient, qkv_sum, out_sum, gain_sum, bias_sum)


def solution(mesh):
    in_specs = (
        P(("grp", "row"), "col", None),
        P(("grp", "row"), "col", None),
        P("row", None),
        P("row", None),
        P(),
        P(),
        P(("grp", "row"), "col"),
    )
    out_specs = (
        P(("grp", "row"), "col", None),
        P(("grp", "row"), None),
        P(("grp", "row"), None),
        P(("grp", "row")),
        P(("grp", "row"), None),
    )
    return jax.shard_map(body, mesh=mesh, in_specs=in_specs, out_specs=out_specs, check_vma=False)
```

```python
import jax
import jax.numpy as jnp
from jax import lax
from jax.sharding import PartitionSpec as P

RAD = 3
HIGHEST = lax.Precision.HIGHEST
HIGH = lax.Precision.HIGH


def extended_2(shard, sides, width):
    for axis, dim in sides:
        devices, length = (lax.axis_size(axis), shard.shape[dim])
        up = [(i, i + 1) for i in range(devices - 1)]
        down = [(j, i) for i, j in up]
        last = lax.slice_in_dim(shard, length - width, length, axis=dim)
        first = lax.slice_in_dim(shard, 0, width, axis=dim)
        before = lax.ppermute(last, axis, up)
        after = lax.ppermute(first, axis, down)
        shard = jnp.concatenate([before, shard, after], axis=dim)
    return shard


def passed_along(value, axis, steps):
    count = lax.axis_size(axis)
    first, last = (max(0, -steps), min(count, count - steps))
    return lax.ppermute(value, axis, [(source, source + steps) for source in range(first, last)])


def gathered_rows(shards):
    count = lax.axis_size("row")
    index = lax.axis_index("row")
    held = [(shards, index)]
    for step in range(2, count, 2):
        pairs = [(r, (r + step) % count) for r in range(count)]
        held.append((lax.ppermute(shards, "row", pairs), (index - step) % count))
    partner = [(r, r ^ 1) for r in range(count)]
    pieces, blocks = [p for p, _ in held], [b for _, b in held]
    swapped = lax.ppermute(tuple(pieces), "row", partner)
    held = held + [(piece, (b ^ 1)) for piece, b in zip(swapped, blocks)]
    outs = []
    for leaf in range(len(shards)):
        size = shards[leaf].shape[0]
        full = jnp.zeros((size * count,) + shards[leaf].shape[1:], shards[leaf].dtype)
        for piece, block in held:
            full = lax.dynamic_update_slice_in_dim(full, piece[leaf], block * size, axis=0)
        outs.append(full)
    return outs


def apply_layer_norm(values, norm_gain_value):
    floats = values.astype(jnp.float32)
    feature_mean = jnp.mean(floats, axis=-1, keepdims=True)
    mean_removed = floats - feature_mean
    variance = jnp.mean(mean_removed * mean_removed, axis=-1, keepdims=True)
    inverse_deviation = lax.rsqrt(variance + 1e-05)
    standardized_input = mean_removed * inverse_deviation
    return (
        (standardized_input * norm_gain_value).astype(jnp.bfloat16),
        standardized_input,
        inverse_deviation,
    )


def window_tables(rows, cols, reach, key_cols):
    side = 2 * reach + 1
    shape = (rows, cols, rows + 2 * reach, key_cols)
    row_gap = lax.broadcasted_iota(jnp.int32, shape, 2) - lax.broadcasted_iota(jnp.int32, shape, 0)
    col_gap = lax.broadcasted_iota(jnp.int32, shape, 3) - lax.broadcasted_iota(jnp.int32, shape, 1)
    inside = (row_gap >= 0) & (row_gap < side) & (col_gap >= 0) & (col_gap < side)
    offset_id = jnp.where(inside, row_gap * side + col_gap, -1)
    centre = (row_gap == reach) & (col_gap == reach)
    nq = rows * cols
    nk = (rows + 2 * reach) * key_cols
    offset_id = offset_id.reshape(nq * nk)
    one_hot = (
        offset_id[None, :] == lax.broadcasted_iota(jnp.int32, (side * side, nq * nk), 0)
    ).astype(jnp.float32)
    return inside.reshape(nq, nk), centre.reshape(nq, nk), one_hot


def body(patches, upstream, qkv_weight, out_weight, layer_norm_gain, pos_bias, valid_mask):
    rows, cols, width = patches.shape
    heads = pos_bias.shape[0]
    hdim = width // heads
    reach = RAD
    ext_rows, ext_cols = rows + 2 * reach, cols + 2 * reach
    key_cols = ext_cols + (-ext_cols) % 8
    nq, nk = rows * cols, ext_rows * key_cols
    scale = float(hdim) ** (-0.5)
    full_qkv, full_out = gathered_rows((qkv_weight, out_weight))
    normed_features, standardized_input, inverse_deviation = apply_layer_norm(
        patches, layer_norm_gain
    )
    flat = normed_features.reshape(-1, width)
    joined = jnp.dot(flat, full_qkv, preferred_element_type=jnp.float32).astype(jnp.bfloat16)
    query = joined[:, :width]
    flags = jnp.broadcast_to(valid_mask.astype(jnp.bfloat16)[:, :, None], (rows, cols, 128))
    kv = jnp.concatenate([joined[:, width:].reshape(rows, cols, 2 * width), flags], axis=-1)
    kv_ext = extended_2(kv, (("row", 0), ("col", 1)), reach)
    kv_ext = jnp.pad(kv_ext, ((0, 0), (0, key_cols - ext_cols), (0, 0))).reshape(nk, 2 * width + 128)
    mask_ext = kv_ext[:, 2 * width]
    q3 = query.reshape(nq, heads, hdim)
    k3 = kv_ext[:, :width].reshape(nk, heads, hdim)
    v3 = kv_ext[:, width : 2 * width].reshape(nk, heads, hdim)

    inside, centre, one_hot = window_tables(rows, cols, reach, key_cols)
    allowed = inside & ((mask_ext[None, :] == 1.0) | centre)
    bias_full = jnp.dot(pos_bias, one_hot, precision=HIGHEST).reshape(heads, nq, nk)
    raw = jnp.einsum("phd,khd->hpk", q3, k3, preferred_element_type=jnp.float32)
    scores = jnp.where(allowed[None], raw * scale + bias_full, -jnp.inf)
    top = jnp.max(scores, axis=-1, keepdims=True)
    expo = jnp.exp(scores - top)
    denom = jnp.sum(expo, axis=-1, keepdims=True)
    probs = expo / denom
    attended3 = jnp.einsum(
        "hpk,khd->phd", probs, v3.astype(jnp.float32), precision=HIGH,
        preferred_element_type=jnp.float32,
    )
    attended = attended3.astype(jnp.bfloat16).reshape(nq, width)

    grad_flat = upstream.reshape(-1, width)
    out_grad = jnp.dot(attended.T, grad_flat, preferred_element_type=jnp.float32)
    out_sum = lax.psum(
        lax.psum_scatter(out_grad.astype(jnp.bfloat16), "row", scatter_dimension=0, tiled=True), "col"
    ).astype(jnp.float32)
    attended_grad = jnp.dot(grad_flat, full_out.T, preferred_element_type=jnp.float32).astype(
        jnp.bfloat16
    )
    ag3 = attended_grad.reshape(nq, heads, hdim)
    delta = jnp.sum(
        ag3.astype(jnp.float32) * attended.reshape(nq, heads, hdim).astype(jnp.float32), axis=-1
    )
    prob_grad = jnp.einsum("phd,khd->hpk", ag3, v3, preferred_element_type=jnp.float32)
    score_grad = probs * (prob_grad - delta.T[:, :, None])
    bias_term = jnp.dot(
        score_grad.reshape(heads, nq * nk), one_hot.T, precision=HIGH,
        preferred_element_type=jnp.float32,
    )
    query_grad = jnp.einsum(
        "hpk,khd->phd", score_grad, k3.astype(jnp.float32), precision=HIGH,
        preferred_element_type=jnp.float32,
    ) * scale
    key_ext_grad = jnp.einsum(
        "hpk,phd->khd", score_grad, q3.astype(jnp.float32), precision=HIGH,
        preferred_element_type=jnp.float32,
    ) * scale
    value_ext_grad = jnp.einsum(
        "hpk,phd->khd", probs, ag3.astype(jnp.float32), precision=HIGH,
        preferred_element_type=jnp.float32,
    )
    buffer = jnp.concatenate(
        [key_ext_grad.reshape(ext_rows, key_cols, width), value_ext_grad.reshape(ext_rows, key_cols, width)],
        axis=-1,
    )[:, :ext_cols]
    from_below = passed_along(buffer[:reach], "row", -1)
    from_above = passed_along(buffer[reach + rows :], "row", 1)
    middle = buffer[reach : reach + rows]
    middle = middle.at[:reach].add(from_above)
    middle = middle.at[rows - reach :].add(from_below)
    from_right = passed_along(middle[:, :reach].astype(jnp.bfloat16), "col", -1).astype(jnp.float32)
    from_left = passed_along(middle[:, reach + cols :].astype(jnp.bfloat16), "col", 1).astype(
        jnp.float32
    )
    inner = middle[:, reach : reach + cols]
    inner = inner.at[:, :reach].add(from_left)
    inner = inner.at[:, cols - reach :].add(from_right)
    joined_grad = jnp.concatenate(
        [query_grad.reshape(rows, cols, width), inner], axis=-1
    ).astype(jnp.bfloat16)
    joined_grad = joined_grad.reshape(-1, 3 * width)
    normed_gradient = jnp.dot(joined_grad, full_qkv.T, preferred_element_type=jnp.float32).reshape(
        rows, cols, width
    )
    gain_product = jnp.sum(normed_gradient * standardized_input, axis=(0, 1))
    scaled_features = normed_gradient * layer_norm_gain
    patch_gradient = upstream.astype(jnp.float32) + inverse_deviation * (
        scaled_features
        - jnp.mean(scaled_features, axis=-1, keepdims=True)
        - standardized_input
        * jnp.mean(scaled_features * standardized_input, axis=-1, keepdims=True)
    )
    row_count = lax.axis_size("row")
    heads_per, rows_per = heads // row_count, width // row_count
    bias_rows = jnp.pad(
        bias_term.reshape(row_count, heads_per, -1), ((0, 0), (0, rows_per - heads_per), (0, 0))
    ).reshape(width, -1)
    offsets = bias_term.shape[1]
    spare = 128 - 1 - offsets
    joined_pad = jnp.pad(joined_grad, ((0, 0), (0, 128)))
    big = jnp.dot(flat.T, joined_pad, preferred_element_type=jnp.float32).astype(jnp.bfloat16)
    extra = jnp.concatenate(
        [gain_product[:, None], bias_rows, jnp.zeros((width, spare), jnp.float32)], axis=1
    ).astype(jnp.bfloat16)
    big = lax.dynamic_update_slice_in_dim(big, extra, 3 * width, axis=1)
    big_sum = lax.psum(lax.psum_scatter(big, "row", scatter_dimension=0, tiled=True), "col")
    big_sum = big_sum.astype(jnp.float32)
    qkv_sum = big_sum[:, : 3 * width]
    gain_sum = big_sum[:, 3 * width]
    bias_sum = big_sum[:heads_per, 3 * width + 1 : 3 * width + 1 + offsets]
    return (patch_gradient, qkv_sum, out_sum, gain_sum, bias_sum)


def solution(mesh):
    in_specs = (
        P(("grp", "row"), "col", None),
        P(("grp", "row"), "col", None),
        P("row", None),
        P("row", None),
        P(),
        P(),
        P(("grp", "row"), "col"),
    )
    out_specs = (
        P(("grp", "row"), "col", None),
        P(("grp", "row"), None),
        P(("grp", "row"), None),
        P(("grp", "row")),
        P(("grp", "row"), None),
    )
    return jax.shard_map(body, mesh=mesh, in_specs=in_specs, out_specs=out_specs, check_vma=False)
```

```python
import jax
import jax.numpy as jnp
from jax import lax
from jax.sharding import PartitionSpec as P

RAD = 3
HIGHEST = lax.Precision.HIGHEST
HIGH = lax.Precision.HIGH


def extended_2(shard, sides, width):
    for axis, dim in sides:
        devices, length = (lax.axis_size(axis), shard.shape[dim])
        up = [(i, i + 1) for i in range(devices - 1)]
        down = [(j, i) for i, j in up]
        last = lax.slice_in_dim(shard, length - width, length, axis=dim)
        first = lax.slice_in_dim(shard, 0, width, axis=dim)
        before = lax.ppermute(last, axis, up)
        after = lax.ppermute(first, axis, down)
        shard = jnp.concatenate([before, shard, after], axis=dim)
    return shard


def passed_along(value, axis, steps):
    count = lax.axis_size(axis)
    first, last = (max(0, -steps), min(count, count - steps))
    return lax.ppermute(value, axis, [(source, source + steps) for source in range(first, last)])


def gathered_rows(shards):
    count = lax.axis_size("row")
    index = lax.axis_index("row")
    held = [(shards, index)]
    for step in range(2, count, 2):
        pairs = [(r, (r + step) % count) for r in range(count)]
        held.append((lax.ppermute(shards, "row", pairs), (index - step) % count))
    partner = [(r, r ^ 1) for r in range(count)]
    pieces, blocks = [p for p, _ in held], [b for _, b in held]
    swapped = lax.ppermute(tuple(pieces), "row", partner)
    held = held + [(piece, (b ^ 1)) for piece, b in zip(swapped, blocks)]
    outs = []
    for leaf in range(len(shards)):
        size = shards[leaf].shape[0]
        full = jnp.zeros((size * count,) + shards[leaf].shape[1:], shards[leaf].dtype)
        for piece, block in held:
            full = lax.dynamic_update_slice_in_dim(full, piece[leaf], block * size, axis=0)
        outs.append(full)
    return outs


def scattered_rows(value):
    count = lax.axis_size("row")
    index = lax.axis_index("row")
    chips = count // 2
    core, chip = index % 2, index // 2
    block = value.shape[0] // count
    grid = value.reshape((chips, 2, block) + value.shape[1:])
    keep = lax.dynamic_index_in_dim(grid, core, axis=1, keepdims=False)
    send = lax.dynamic_index_in_dim(grid, 1 - core, axis=1, keepdims=False)
    recv = lax.ppermute(send, "row", [(r, r ^ 1) for r in range(count)])
    summed = keep.astype(jnp.float32) + recv.astype(jnp.float32)
    total = lax.dynamic_index_in_dim(summed, chip, axis=0, keepdims=False)
    shipped = summed.astype(value.dtype)
    for step in range(1, chips):
        piece = lax.dynamic_index_in_dim(shipped, (chip + step) % chips, axis=0, keepdims=False)
        pairs = [(r, (r + 2 * step) % count) for r in range(count)]
        total = total + lax.ppermute(piece, "row", pairs).astype(jnp.float32)
    return total


def apply_layer_norm(values, norm_gain_value):
    floats = values.astype(jnp.float32)
    feature_mean = jnp.mean(floats, axis=-1, keepdims=True)
    mean_removed = floats - feature_mean
    variance = jnp.mean(mean_removed * mean_removed, axis=-1, keepdims=True)
    inverse_deviation = lax.rsqrt(variance + 1e-05)
    standardized_input = mean_removed * inverse_deviation
    return (
        (standardized_input * norm_gain_value).astype(jnp.bfloat16),
        standardized_input,
        inverse_deviation,
    )


def window_tables(rows, cols, reach, key_cols):
    side = 2 * reach + 1
    shape = (rows, cols, rows + 2 * reach, key_cols)
    row_gap = lax.broadcasted_iota(jnp.int32, shape, 2) - lax.broadcasted_iota(jnp.int32, shape, 0)
    col_gap = lax.broadcasted_iota(jnp.int32, shape, 3) - lax.broadcasted_iota(jnp.int32, shape, 1)
    inside = (row_gap >= 0) & (row_gap < side) & (col_gap >= 0) & (col_gap < side)
    offset_id = jnp.where(inside, row_gap * side + col_gap, -1)
    centre = (row_gap == reach) & (col_gap == reach)
    nq = rows * cols
    nk = (rows + 2 * reach) * key_cols
    offset_id = offset_id.reshape(nq * nk)
    one_hot = (
        offset_id[None, :] == lax.broadcasted_iota(jnp.int32, (side * side, nq * nk), 0)
    ).astype(jnp.float32)
    return inside.reshape(nq, nk), centre.reshape(nq, nk), one_hot


def body(patches, upstream, qkv_weight, out_weight, layer_norm_gain, pos_bias, valid_mask):
    rows, cols, width = patches.shape
    heads = pos_bias.shape[0]
    hdim = width // heads
    reach = RAD
    ext_rows, ext_cols = rows + 2 * reach, cols + 2 * reach
    key_cols = ext_cols + (-ext_cols) % 8
    nq, nk = rows * cols, ext_rows * key_cols
    scale = float(hdim) ** (-0.5)
    full_qkv, full_out = gathered_rows((qkv_weight, out_weight))
    normed_features, standardized_input, inverse_deviation = apply_layer_norm(
        patches, layer_norm_gain
    )
    flat = normed_features.reshape(-1, width)
    joined = jnp.dot(flat, full_qkv, preferred_element_type=jnp.float32).astype(jnp.bfloat16)
    query = joined[:, :width]
    flags = jnp.broadcast_to(valid_mask.astype(jnp.bfloat16)[:, :, None], (rows, cols, 128))
    kv = jnp.concatenate([joined[:, width:].reshape(rows, cols, 2 * width), flags], axis=-1)
    kv_ext = extended_2(kv, (("row", 0), ("col", 1)), reach)
    kv_ext = jnp.pad(kv_ext, ((0, 0), (0, key_cols - ext_cols), (0, 0))).reshape(nk, 2 * width + 128)
    mask_ext = kv_ext[:, 2 * width]
    q3 = query.reshape(nq, heads, hdim)
    k3 = kv_ext[:, :width].reshape(nk, heads, hdim)
    v3 = kv_ext[:, width : 2 * width].reshape(nk, heads, hdim)

    inside, centre, one_hot = window_tables(rows, cols, reach, key_cols)
    allowed = inside & ((mask_ext[None, :] == 1.0) | centre)
    bias_full = jnp.dot(pos_bias, one_hot, precision=HIGHEST).reshape(heads, nq, nk)
    raw = jnp.einsum("phd,khd->hpk", q3, k3, preferred_element_type=jnp.float32)
    scores = jnp.where(allowed[None], raw * scale + bias_full, -jnp.inf)
    top = jnp.max(scores, axis=-1, keepdims=True)
    expo = jnp.exp(scores - top)
    denom = jnp.sum(expo, axis=-1, keepdims=True)
    probs = expo / denom
    attended3 = jnp.einsum(
        "hpk,khd->phd", probs, v3.astype(jnp.float32), precision=HIGH,
        preferred_element_type=jnp.float32,
    )
    attended = attended3.astype(jnp.bfloat16).reshape(nq, width)

    grad_flat = upstream.reshape(-1, width)
    out_grad = jnp.dot(attended.T, grad_flat, preferred_element_type=jnp.float32)
    out_sum = lax.psum(
        lax.psum_scatter(out_grad.astype(jnp.bfloat16), "row", scatter_dimension=0, tiled=True), "col"
    ).astype(jnp.float32)
    attended_grad = jnp.dot(grad_flat, full_out.T, preferred_element_type=jnp.float32).astype(
        jnp.bfloat16
    )
    ag3 = attended_grad.reshape(nq, heads, hdim)
    delta = jnp.sum(
        ag3.astype(jnp.float32) * attended.reshape(nq, heads, hdim).astype(jnp.float32), axis=-1
    )
    prob_grad = jnp.einsum("phd,khd->hpk", ag3, v3, preferred_element_type=jnp.float32)
    score_grad = probs * (prob_grad - delta.T[:, :, None])
    bias_term = jnp.dot(
        score_grad.reshape(heads, nq * nk), one_hot.T, precision=HIGH,
        preferred_element_type=jnp.float32,
    )
    query_grad = jnp.einsum(
        "hpk,khd->phd", score_grad, k3.astype(jnp.float32), precision=HIGH,
        preferred_element_type=jnp.float32,
    ) * scale
    key_ext_grad = jnp.einsum(
        "hpk,phd->khd", score_grad, q3.astype(jnp.float32), precision=HIGH,
        preferred_element_type=jnp.float32,
    ) * scale
    value_ext_grad = jnp.einsum(
        "hpk,phd->khd", probs, ag3.astype(jnp.float32), precision=HIGH,
        preferred_element_type=jnp.float32,
    )
    buffer = jnp.concatenate(
        [key_ext_grad.reshape(ext_rows, key_cols, width), value_ext_grad.reshape(ext_rows, key_cols, width)],
        axis=-1,
    )[:, :ext_cols]
    from_below = passed_along(buffer[:reach], "row", -1)
    from_above = passed_along(buffer[reach + rows :], "row", 1)
    middle = buffer[reach : reach + rows]
    middle = middle.at[:reach].add(from_above)
    middle = middle.at[rows - reach :].add(from_below)
    from_right = passed_along(middle[:, :reach].astype(jnp.bfloat16), "col", -1).astype(jnp.float32)
    from_left = passed_along(middle[:, reach + cols :].astype(jnp.bfloat16), "col", 1).astype(
        jnp.float32
    )
    inner = middle[:, reach : reach + cols]
    inner = inner.at[:, :reach].add(from_left)
    inner = inner.at[:, cols - reach :].add(from_right)
    joined_grad = jnp.concatenate(
        [query_grad.reshape(rows, cols, width), inner], axis=-1
    ).astype(jnp.bfloat16)
    joined_grad = joined_grad.reshape(-1, 3 * width)
    normed_gradient = jnp.dot(joined_grad, full_qkv.T, preferred_element_type=jnp.float32).reshape(
        rows, cols, width
    )
    gain_product = jnp.sum(normed_gradient * standardized_input, axis=(0, 1))
    scaled_features = normed_gradient * layer_norm_gain
    patch_gradient = upstream.astype(jnp.float32) + inverse_deviation * (
        scaled_features
        - jnp.mean(scaled_features, axis=-1, keepdims=True)
        - standardized_input
        * jnp.mean(scaled_features * standardized_input, axis=-1, keepdims=True)
    )
    row_count = lax.axis_size("row")
    heads_per, rows_per = heads // row_count, width // row_count
    bias_rows = jnp.pad(
        bias_term.reshape(row_count, heads_per, -1), ((0, 0), (0, rows_per - heads_per), (0, 0))
    ).reshape(width, -1)
    offsets = bias_term.shape[1]
    spare = 128 - 1 - offsets
    joined_pad = jnp.pad(joined_grad, ((0, 0), (0, 128)))
    big = jnp.dot(flat.T, joined_pad, preferred_element_type=jnp.float32).astype(jnp.bfloat16)
    extra = jnp.concatenate(
        [gain_product[:, None], bias_rows, jnp.zeros((width, spare), jnp.float32)], axis=1
    ).astype(jnp.bfloat16)
    big = lax.dynamic_update_slice_in_dim(big, extra, 3 * width, axis=1)
    big_sum = lax.psum(scattered_rows(big).astype(jnp.bfloat16), "col")
    big_sum = big_sum.astype(jnp.float32)
    qkv_sum = big_sum[:, : 3 * width]
    gain_sum = big_sum[:, 3 * width]
    bias_sum = big_sum[:heads_per, 3 * width + 1 : 3 * width + 1 + offsets]
    return (patch_gradient, qkv_sum, out_sum, gain_sum, bias_sum)


def solution(mesh):
    in_specs = (
        P(("grp", "row"), "col", None),
        P(("grp", "row"), "col", None),
        P("row", None),
        P("row", None),
        P(),
        P(),
        P(("grp", "row"), "col"),
    )
    out_specs = (
        P(("grp", "row"), "col", None),
        P(("grp", "row"), None),
        P(("grp", "row"), None),
        P(("grp", "row")),
        P(("grp", "row"), None),
    )
    return jax.shard_map(body, mesh=mesh, in_specs=in_specs, out_specs=out_specs, check_vma=False)
```
